32 devices in a mesh: group: 16 (over z, x, core), loop: 2 (over y).
Axes of the slice: x: 2, y: 2, z: 4, core: 2. Of those that a mesh axis runs over, the one named last changes fastest.
Arguments:
- user_factors: bfloat16 [32768, 256], P('group'), may hold values from -1.5 to 1.5
- item_factors: bfloat16 [2048, 256], P('loop'), may hold values from -1.5 to 1.5
- tag_factors: bfloat16 [2048, 256], P('group'), may hold values from -1.5 to 1.5
- ratings: bfloat16 [32768, 2048], P('group', 'loop'), may hold values from -6 to 6
- rating_tiles: int32 [256, 16], P('group', 'loop'), may hold values 0 or 1
- tag_links: bfloat16 [2048, 2048], P('loop', 'group'), may hold values from -6 to 6
- link_tiles: int32 [16, 16], P('loop', 'group'), may hold values 0 or 1
Outputs:
- new_users: bfloat16 [32768, 256], P('group')
- new_items: bfloat16 [2048, 256], P('loop')
- new_tags: bfloat16 [2048, 256], P('group')
The draws below stay inside these ranges and needn't reach their ends.
Inputs may be any that keep to these rules, and one draw needn't show every extreme that they name: `rating_tiles`: 1 marks a tile of observed entries, 0 an empty tile. `link_tiles`: 1 marks a tile of observed entries, 0 an empty tile.
All inputs are finite; a program needn't handle non-finite values. No bound on the sum of `rating_tiles` or of `link_tiles` on one device may be relied on, other than what follows from the above.
Results may differ from the reference program's by a relative error of at most 0.0034.
Values may be sent and summed in bfloat16 or wider, within the bound.
No kernel may reach another device: no remote copies, remote signals or barrier semaphores. Data moves between devices by JAX's collectives and lax.ppermute only.
A program may use at most 64 MiB of HBM per device.

```python
import jax
import jax.numpy as jnp
from jax import lax

RANK = 256
USER_DEV = 2048
USERS = 32768
ITEMS = 2048
TAGS = 2048
N_GROUP = 16


def place_ends(result, own_key, least, top_value):
    dims = result.shape
    place = [jax.random.randint(jax.random.fold_in(own_key, axis), (), 0, dims[axis]) for axis in range(len(dims))]
    result = result.at[tuple(place)].set(least)
    longest = dims.index(max(dims))
    place[longest] = (place[longest] + 1) % dims[longest]
    return result.at[tuple(place)].set(top_value)


def steps_of(rng, dims, cuts, smallest, high):
    level, own = 1.0, jax.random.fold_in(rng, 6)
    for axis_at, blocks in cuts:
        steps = jnp.exp(jax.random.uniform(jax.random.fold_in(own, axis_at), (blocks,), jnp.float32, smallest / len(cuts), high / len(cuts)))
        level = level * jnp.repeat(steps, dims[axis_at] // blocks).reshape([-1 if axis == axis_at else 1 for axis in range(len(dims))])
    return level


def gaussian(rng, shape, spread, reach, shards=(), dtype=jnp.bfloat16):
    loudness = steps_of(rng, shape, shards, -0.22, 0.18) if shards else 1.0
    result = jax.random.normal(rng, shape, jnp.float32) * spread * loudness
    return jnp.minimum(jnp.maximum(result, -reach), reach).astype(dtype)


def setup_inputs(seed: int = 0) -> dict:
    streams_of = jax.random.split(jax.random.key(seed), 8)
    return {
        "user_factors": gaussian(streams_of[0], (USERS, RANK), (RANK ** -0.25), 1.5, ((0, 16),)),
        "item_factors": gaussian(streams_of[1], (ITEMS, RANK), (RANK ** -0.25), 1.5, ((0, 2),)),
        "tag_factors": gaussian(streams_of[2], (TAGS, RANK), (RANK ** -0.25), 1.5, ((0, 16),)),
        "ratings": gaussian(streams_of[3], (USERS, ITEMS), 1.0, 6.0, ((0, 16), (1, 2))),
        "rating_tiles": place_ends((jax.random.randint(streams_of[4], (USERS // 128, ITEMS // 128), 0, 2) < 1).astype(jnp.int32), jax.random.fold_in(streams_of[4], 1), 0, 1),
        "tag_links": gaussian(streams_of[5], (ITEMS, TAGS), 1.0, 6.0, ((0, 2), (1, 16))),
        "link_tiles": place_ends((jax.random.randint(streams_of[6], (ITEMS // 128, TAGS // 128), 0, 2) < 1).astype(jnp.int32), jax.random.fold_in(streams_of[6], 1), 0, 1),
    }


step_users = 0.015
step_items = 0.004
step_tags = 0.015


def tile_masked(values, tile_flags):
    height, breadth = values.shape
    blocks = values.reshape(height // 128, 128, breadth // 128, 128)
    masked = blocks * tile_flags.astype(jnp.float32)[:, None, :, None]
    return masked.reshape(height, breadth)


def residual_of(observed, row_factors, column_factors, tile_flags):
    predicted = lax.dot_general(row_factors, column_factors, (((1,), (1,)), ((), ())), preferred_element_type=jnp.float32)
    return tile_masked(observed.astype(jnp.float32) - predicted, tile_flags).astype(jnp.bfloat16)


def transposed_product(first_operand, second_operand):
    return lax.dot_general(first_operand, second_operand, (((0,), (0,)), ((), ())), preferred_element_type=jnp.float32)


def reference(user_factors, item_factors, tag_factors, ratings, rating_tiles, tag_links, link_tiles):
    user_blocks = user_factors.reshape(N_GROUP, USER_DEV, RANK)
    rating_blocks = ratings.reshape(N_GROUP, USER_DEV, ITEMS)
    flag_blocks = rating_tiles.reshape(N_GROUP, USER_DEV // 128, ITEMS // 128)

    def visit(carried, inputs):
        users_here, observed, flags_here = inputs
        errors = residual_of(observed, users_here, item_factors, flags_here)
        user_grad = jnp.dot(errors, item_factors, preferred_element_type=jnp.float32)
        carried = carried + transposed_product(errors, users_here)
        fresh = (users_here.astype(jnp.float32) + step_users * user_grad).astype(jnp.bfloat16)
        return carried, fresh

    start_grad = jnp.zeros((ITEMS, RANK), jnp.float32)
    item_grad, fresh_users = lax.scan(visit, start_grad, (user_blocks, rating_blocks, flag_blocks))
    link_errors = residual_of(tag_links, item_factors, tag_factors, link_tiles)
    item_grad = item_grad + jnp.dot(link_errors, tag_factors, preferred_element_type=jnp.float32)
    tag_grad = transposed_product(link_errors, item_factors)
    new_items = (item_factors.astype(jnp.float32) + step_items * item_grad).astype(jnp.bfloat16)
    new_tags = (tag_factors.astype(jnp.float32) + step_tags * tag_grad).astype(jnp.bfloat16)
    return (fresh_users.reshape(USERS, RANK), new_items, new_tags)
```

```python
import jax
import jax.numpy as jnp
from jax import lax
from jax.sharding import PartitionSpec as P

step_users = 0.015
step_items = 0.004
step_tags = 0.015


def tile_masked(values, tile_flags):
    height, breadth = values.shape
    blocks = values.reshape(height // 128, 128, breadth // 128, 128)
    masked = blocks * tile_flags.astype(jnp.float32)[:, None, :, None]
    return masked.reshape(height, breadth)


def residual_of(observed, row_factors, column_factors, tile_flags):
    predicted = lax.dot_general(
        row_factors, column_factors, (((1,), (1,)), ((), ())), preferred_element_type=jnp.float32
    )
    return tile_masked(observed.astype(jnp.float32) - predicted, tile_flags).astype(jnp.bfloat16)


def transposed_product(first_operand, second_operand):
    return lax.dot_general(
        first_operand, second_operand, (((0,), (0,)), ((), ())), preferred_element_type=jnp.float32
    )


def advance(factors, gradient, rate):
    return (factors.astype(jnp.float32) + rate * gradient).astype(jnp.bfloat16)


def xor_pairs(count, bit):
    return [(i, i ^ (1 << bit)) for i in range(count)]


def halving_scatter(parts, axis, count, position):
    steps = count.bit_length() - 1
    offsets = [0 for _ in parts]
    for bit in range(steps):
        side = (position >> bit) & 1
        halves = [p.shape[0] // 2 for p in parts]
        kept = [lax.dynamic_slice_in_dim(p, side * h, h, 0) for p, h in zip(parts, halves)]
        sent = [lax.dynamic_slice_in_dim(p, (1 - side) * h, h, 0) for p, h in zip(parts, halves)]
        got = lax.ppermute(tuple(sent), axis, xor_pairs(count, bit))
        parts = [k + g for k, g in zip(kept, got)]
        offsets = [o + side * h for o, h in zip(offsets, halves)]
    return parts, offsets


def doubling_gather(parts, axis, count, position):
    steps = count.bit_length() - 1
    for bit in reversed(range(steps)):
        side = (position >> bit) & 1
        got = lax.ppermute(tuple(parts), axis, xor_pairs(count, bit))
        parts = [
            jnp.where(side == 0, jnp.concatenate([m, g], 0), jnp.concatenate([g, m], 0))
            for m, g in zip(parts, got)
        ]
    return parts


def shards(user_factors, item_factors, tag_factors, ratings, rating_tiles, tag_links, link_tiles):
    group_count = lax.axis_size("group")
    loop_count = lax.axis_size("loop")
    group_position = lax.axis_index("group")
    loop_position = lax.axis_index("loop")

    link_errors = residual_of(tag_links, item_factors, tag_factors, link_tiles)
    rating_errors = residual_of(ratings, user_factors, item_factors, rating_tiles)
    user_part = jnp.dot(rating_errors, item_factors, preferred_element_type=jnp.float32)
    tag_part = transposed_product(link_errors, item_factors)
    item_part = transposed_product(rating_errors, user_factors) + jnp.dot(
        link_errors, tag_factors, preferred_element_type=jnp.float32
    )

    (user_share, tag_share), (user_offset, tag_offset) = halving_scatter(
        [user_part, tag_part], "loop", loop_count, loop_position
    )
    fresh_users = advance(
        lax.dynamic_slice_in_dim(user_factors, user_offset, user_share.shape[0], 0),
        user_share,
        step_users,
    )
    fresh_tags = advance(
        lax.dynamic_slice_in_dim(tag_factors, tag_offset, tag_share.shape[0], 0),
        tag_share,
        step_tags,
    )
    new_users, new_tags = doubling_gather(
        [fresh_users, fresh_tags], "loop", loop_count, loop_position
    )

    (item_share,), (item_offset,) = halving_scatter([item_part], "group", group_count, group_position)
    fresh_items = advance(
        lax.dynamic_slice_in_dim(item_factors, item_offset, item_share.shape[0], 0),
        item_share,
        step_items,
    )
    (new_items,) = doubling_gather([fresh_items], "group", group_count, group_position)
    return (new_users, new_items, new_tags)


def solution(mesh):
    in_specs = (
        P("group", None),
        P("loop", None),
        P("group", None),
        P("group", "loop"),
        P("group", "loop"),
        P("loop", "group"),
        P("loop", "group"),
    )
    out_specs = (P("group", None), P("loop", None), P("group", None))
    return jax.shard_map(shards, mesh=mesh, in_specs=in_specs, out_specs=out_specs, check_vma=False)
```

```python
import jax
import jax.numpy as jnp
from jax import lax
from jax.sharding import PartitionSpec as P

step_users = 0.015
step_items = 0.004
step_tags = 0.015


def tile_masked(values, tile_flags):
    height, breadth = values.shape
    blocks = values.reshape(height // 128, 128, breadth // 128, 128)
    masked = blocks * tile_flags.astype(jnp.float32)[:, None, :, None]
    return masked.reshape(height, breadth)


def residual_of(observed, row_factors, column_factors, tile_flags):
    predicted = lax.dot_general(
        row_factors, column_factors, (((1,), (1,)), ((), ())), preferred_element_type=jnp.float32
    )
    return tile_masked(observed.astype(jnp.float32) - predicted, tile_flags).astype(jnp.bfloat16)


def transposed_product(first_operand, second_operand):
    return lax.dot_general(
        first_operand, second_operand, (((0,), (0,)), ((), ())), preferred_element_type=jnp.float32
    )


def advance(factors, gradient, rate):
    return (factors.astype(jnp.float32) + rate * gradient).astype(jnp.bfloat16)


def xor_pairs(count, bit):
    return [(i, i ^ (1 << bit)) for i in range(count)]


def halving_scatter(parts, axis, count, position):
    steps = count.bit_length() - 1
    offsets = [0 for _ in parts]
    for bit in range(steps):
        side = (position >> bit) & 1
        halves = [p.shape[0] // 2 for p in parts]
        kept = [lax.dynamic_slice_in_dim(p, side * h, h, 0) for p, h in zip(parts, halves)]
        sent = [lax.dynamic_slice_in_dim(p, (1 - side) * h, h, 0) for p, h in zip(parts, halves)]
        got = lax.ppermute(tuple(sent), axis, xor_pairs(count, bit))
        parts = [k + g for k, g in zip(kept, got)]
        offsets = [o + side * h for o, h in zip(offsets, halves)]
    return parts, offsets


def doubling_gather(parts, axis, count, position):
    steps = count.bit_length() - 1
    for bit in reversed(range(steps)):
        side = (position >> bit) & 1
        got = lax.ppermute(tuple(parts), axis, xor_pairs(count, bit))
        parts = [
            jnp.where(side == 0, jnp.concatenate([m, g], 0), jnp.concatenate([g, m], 0))
            for m, g in zip(parts, got)
        ]
    return parts


def spread_scatter(part, axis, count):
    rows = part.shape[0] // count
    pieces = part.reshape(count, rows, part.shape[1])
    pieces = lax.all_to_all(pieces, axis, 0, 0, tiled=False)
    return jnp.sum(pieces, axis=0)


def spread_gather(share, axis, count):
    pieces = jnp.broadcast_to(share[None], (count,) + share.shape)
    pieces = lax.all_to_all(pieces, axis, 0, 0, tiled=False)
    return pieces.reshape(count * share.shape[0], share.shape[1])


def shards(user_factors, item_factors, tag_factors, ratings, rating_tiles, tag_links, link_tiles):
    group_count = lax.axis_size("group")
    loop_count = lax.axis_size("loop")
    group_position = lax.axis_index("group")
    loop_position = lax.axis_index("loop")

    link_errors = residual_of(tag_links, item_factors, tag_factors, link_tiles)
    rating_errors = residual_of(ratings, user_factors, item_factors, rating_tiles)
    user_part = jnp.dot(rating_errors, item_factors, preferred_element_type=jnp.float32)
    tag_part = transposed_product(link_errors, item_factors)
    user_part, tag_part, rating_errors, link_errors = lax.optimization_barrier(
        (user_part, tag_part, rating_errors, link_errors)
    )

    (user_share, tag_share), (user_offset, tag_offset) = halving_scatter(
        [user_part, tag_part], "loop", loop_count, loop_position
    )
    fresh_users = advance(
        lax.dynamic_slice_in_dim(user_factors, user_offset, user_share.shape[0], 0),
        user_share,
        step_users,
    )
    fresh_tags = advance(
        lax.dynamic_slice_in_dim(tag_factors, tag_offset, tag_share.shape[0], 0),
        tag_share,
        step_tags,
    )
    new_users, new_tags = doubling_gather(
        [fresh_users, fresh_tags], "loop", loop_count, loop_position
    )

    item_part = transposed_product(rating_errors, user_factors) + jnp.dot(
        link_errors, tag_factors, preferred_element_type=jnp.float32
    )
    item_share = spread_scatter(item_part, "group", group_count)
    share_rows = item_share.shape[0]
    fresh_items = advance(
        lax.dynamic_slice_in_dim(item_factors, group_position * share_rows, share_rows, 0),
        item_share,
        step_items,
    )
    new_items = spread_gather(fresh_items, "group", group_count)
    return (new_users, new_items, new_tags)


def solution(mesh):
    in_specs = (
        P("group", None),
        P("loop", None),
        P("group", None),
        P("group", "loop"),
        P("group", "loop"),
        P("loop", "group"),
        P("loop", "group"),
    )
    out_specs = (P("group", None), P("loop", None), P("group", None))
    return jax.shard_map(shards, mesh=mesh, in_specs=in_specs, out_specs=out_specs, check_vma=False)
```

```python
import jax
import jax.numpy as jnp
from jax import lax
from jax.sharding import PartitionSpec as P

step_users = 0.015
step_items = 0.004
step_tags = 0.015


def tile_masked(values, tile_flags):
    height, breadth = values.shape
    blocks = values.reshape(height // 128, 128, breadth // 128, 128)
    masked = blocks * tile_flags.astype(jnp.float32)[:, None, :, None]
    return masked.reshape(height, breadth)


def residual_of(observed, row_factors, column_factors, tile_flags):
    predicted = lax.dot_general(
        row_factors, column_factors, (((1,), (1,)), ((), ())), preferred_element_type=jnp.float32
    )
    return tile_masked(observed.astype(jnp.float32) - predicted, tile_flags).astype(jnp.bfloat16)


def transposed_product(first_operand, second_operand):
    return lax.dot_general(
        first_operand, second_operand, (((0,), (0,)), ((), ())), preferred_element_type=jnp.float32
    )


def advance(factors, gradient, rate):
    return (factors.astype(jnp.float32) + rate * gradient).astype(jnp.bfloat16)


def xor_pairs(count, bit):
    return [(i, i ^ (1 << bit)) for i in range(count)]


def halving_scatter(parts, axis, count, position):
    steps = count.bit_length() - 1
    offsets = [0 for _ in parts]
    for bit in range(steps):
        side = (position >> bit) & 1
        halves = [p.shape[0] // 2 for p in parts]
        kept = [lax.dynamic_slice_in_dim(p, side * h, h, 0) for p, h in zip(parts, halves)]
        sent = [lax.dynamic_slice_in_dim(p, (1 - side) * h, h, 0) for p, h in zip(parts, halves)]
        got = lax.ppermute(tuple(sent), axis, xor_pairs(count, bit))
        parts = [k + g for k, g in zip(kept, got)]
        offsets = [o + side * h for o, h in zip(offsets, halves)]
    return parts, offsets


def doubling_gather(parts, axis, count, position):
    steps = count.bit_length() - 1
    for bit in reversed(range(steps)):
        side = (position >> bit) & 1
        got = lax.ppermute(tuple(parts), axis, xor_pairs(count, bit))
        parts = [
            jnp.where(side == 0, jnp.concatenate([m, g], 0), jnp.concatenate([g, m], 0))
            for m, g in zip(parts, got)
        ]
    return parts


def shards(user_factors, item_factors, tag_factors, ratings, rating_tiles, tag_links, link_tiles):
    group_count = lax.axis_size("group")
    loop_count = lax.axis_size("loop")
    group_position = lax.axis_index("group")
    loop_position = lax.axis_index("loop")

    link_errors = residual_of(tag_links, item_factors, tag_factors, link_tiles)
    rating_errors = residual_of(ratings, user_factors, item_factors, rating_tiles)
    user_part = jnp.dot(rating_errors, item_factors, preferred_element_type=jnp.float32)
    tag_part = transposed_product(link_errors, item_factors)
    joint_part = jnp.concatenate([user_part, tag_part], 0)

    joint_part, rating_errors, link_errors = lax.optimization_barrier(
        (joint_part, rating_errors, link_errors)
    )
    (joint_share,), (joint_offset,) = halving_scatter(
        [joint_part], "loop", loop_count, loop_position
    )
    item_part = transposed_product(rating_errors, user_factors) + jnp.dot(
        link_errors, tag_factors, preferred_element_type=jnp.float32
    )
    joint_factors = jnp.concatenate([user_factors, tag_factors], 0)
    fresh_joint = advance(
        lax.dynamic_slice_in_dim(joint_factors, joint_offset, joint_share.shape[0], 0),
        joint_share,
        jnp.where(
            joint_offset + jnp.arange(joint_share.shape[0])[:, None] < user_factors.shape[0],
            step_users,
            step_tags,
        ),
    )
    (new_joint,) = doubling_gather([fresh_joint], "loop", loop_count, loop_position)
    new_users = new_joint[: user_factors.shape[0]]
    new_tags = new_joint[user_factors.shape[0] :]

    (item_share,), (item_offset,) = halving_scatter([item_part], "group", group_count, group_position)
    fresh_items = advance(
        lax.dynamic_slice_in_dim(item_factors, item_offset, item_share.shape[0], 0),
        item_share,
        step_items,
    )
    (new_items,) = doubling_gather([fresh_items], "group", group_count, group_position)
    return (new_users, new_items, new_tags)


def solution(mesh):
    in_specs = (
        P("group", None),
        P("loop", None),
        P("group", None),
        P("group", "loop"),
        P("group", "loop"),
        P("loop", "group"),
        P("loop", "group"),
    )
    out_specs = (P("group", None), P("loop", None), P("group", None))
    return jax.shard_map(shards, mesh=mesh, in_specs=in_specs, out_specs=out_specs, check_vma=False)
```

```python
import jax
import jax.numpy as jnp
from jax import lax
from jax.sharding import PartitionSpec as P

step_users = 0.015
step_items = 0.004
step_tags = 0.015


def tile_masked(values, tile_flags):
    height, breadth = values.shape
    blocks = values.reshape(height // 128, 128, breadth // 128, 128)
    masked = blocks * tile_flags.astype(jnp.float32)[:, None, :, None]
    return masked.reshape(height, breadth)


def residual_of(observed, row_factors, column_factors, tile_flags):
    predicted = lax.dot_general(
        row_factors, column_factors, (((1,), (1,)), ((), ())), preferred_element_type=jnp.float32
    )
    return tile_masked(observed.astype(jnp.float32) - predicted, tile_flags).astype(jnp.bfloat16)


def transposed_product(first_operand, second_operand):
    return lax.dot_general(
        first_operand, second_operand, (((0,), (0,)), ((), ())), preferred_element_type=jnp.float32
    )


def advance(factors, gradient, rate):
    return (factors.astype(jnp.float32) + rate * gradient).astype(jnp.bfloat16)


def xor_pairs(count, bit, mask=0):
    mask = mask or (1 << bit)
    return [(i, i ^ mask) for i in range(count)]


def halving_scatter(parts, axis, count, position):
    steps = count.bit_length() - 1
    offsets = [0 for _ in parts]
    for bit in range(steps):
        side = (position >> bit) & 1
        halves = [p.shape[0] // 2 for p in parts]
        kept = [lax.dynamic_slice_in_dim(p, side * h, h, 0) for p, h in zip(parts, halves)]
        sent = [lax.dynamic_slice_in_dim(p, (1 - side) * h, h, 0) for p, h in zip(parts, halves)]
        got = lax.ppermute(tuple(sent), axis, xor_pairs(count, bit))
        parts = [k + g for k, g in zip(kept, got)]
        offsets = [o + side * h for o, h in zip(offsets, halves)]
    return parts, offsets


def doubling_gather(parts, axis, count, position):
    steps = count.bit_length() - 1
    for bit in reversed(range(steps)):
        side = (position >> bit) & 1
        got = lax.ppermute(tuple(parts), axis, xor_pairs(count, bit))
        parts = [
            jnp.where(side == 0, jnp.concatenate([m, g], 0), jnp.concatenate([g, m], 0))
            for m, g in zip(parts, got)
        ]
    return parts


def radix_stages(count):
    bits = count.bit_length() - 1
    stages = []
    low = 0
    while low < bits:
        width = 1 if low == 0 else min(3, bits - low)
        stages.append((low, width))
        low += width
    return stages


def radix_scatter(part, axis, count, position, stages):
    offset = 0
    for low, width in stages:
        radix = 1 << width
        local = (position >> low) & (radix - 1)
        rows = part.shape[0] // radix
        total = lax.dynamic_slice_in_dim(part, local * rows, rows, 0)
        for shift in range(1, radix):
            sent = lax.dynamic_slice_in_dim(part, (local ^ shift) * rows, rows, 0)
            total = total + lax.ppermute(sent, axis, xor_pairs(count, 0, shift << low))
        part = total
        offset = offset + local * rows
    return part, offset


def radix_gather(share, axis, count, position, stages):
    for low, width in reversed(stages):
        radix = 1 << width
        local = (position >> low) & (radix - 1)
        pieces = [share] + [
            lax.ppermute(share, axis, xor_pairs(count, 0, shift << low))
            for shift in range(1, radix)
        ]
        stacked = jnp.stack(pieces, 0)
        share = jnp.concatenate(
            [lax.dynamic_index_in_dim(stacked, local ^ block, 0, False) for block in range(radix)],
            0,
        )
    return share


def loop_pair_step(user_factors, item_factors, tag_factors, rating_errors, link_errors, position):
    user_half = user_factors.shape[0] // 2
    tag_half = tag_factors.shape[0] // 2
    side = position & 1

    def partial(rows_side):
        users = jnp.dot(
            lax.dynamic_slice_in_dim(rating_errors, rows_side * user_half, user_half, 0),
            item_factors,
            preferred_element_type=jnp.float32,
        )
        tags = transposed_product(
            lax.dynamic_slice_in_dim(link_errors, rows_side * tag_half, tag_half, 1),
            item_factors,
        )
        return jnp.concatenate([users, tags], 0)

    sent = partial(1 - side)
    sent, rating_errors, link_errors = lax.optimization_barrier((sent, rating_errors, link_errors))
    got = lax.ppermute(sent, "loop", [(0, 1), (1, 0)])
    total = partial(side) + got
    fresh = jnp.concatenate(
        [
            advance(
                lax.dynamic_slice_in_dim(user_factors, side * user_half, user_half, 0),
                total[:user_half],
                step_users,
            ),
            advance(
                lax.dynamic_slice_in_dim(tag_factors, side * tag_half, tag_half, 0),
                total[user_half:],
                step_tags,
            ),
        ],
        0,
    )
    other = lax.ppermute(fresh, "loop", [(0, 1), (1, 0)])
    low = jnp.where(side == 0, fresh, other)
    high = jnp.where(side == 0, other, fresh)
    new_users = jnp.concatenate([low[:user_half], high[:user_half]], 0)
    new_tags = jnp.concatenate([low[user_half:], high[user_half:]], 0)
    return new_users, new_tags, rating_errors, link_errors, got


def shards(user_factors, item_factors, tag_factors, ratings, rating_tiles, tag_links, link_tiles):
    group_count = lax.axis_size("group")
    loop_count = lax.axis_size("loop")
    group_position = lax.axis_index("group")
    loop_position = lax.axis_index("loop")

    link_errors = residual_of(tag_links, item_factors, tag_factors, link_tiles)
    rating_errors = residual_of(ratings, user_factors, item_factors, rating_tiles)
    if loop_count == 2:
        new_users, new_tags, rating_errors, link_errors, got = loop_pair_step(
            user_factors, item_factors, tag_factors, rating_errors, link_errors, loop_position
        )
    else:
        got = None
        user_part = jnp.dot(rating_errors, item_factors, preferred_element_type=jnp.float32)
        tag_part = transposed_product(link_errors, item_factors)
        (user_share, tag_share), (user_offset, tag_offset) = halving_scatter(
            [user_part, tag_part], "loop", loop_count, loop_position
        )
        fresh_users = advance(
            lax.dynamic_slice_in_dim(user_factors, user_offset, user_share.shape[0], 0),
            user_share,
            step_users,
        )
        fresh_tags = advance(
            lax.dynamic_slice_in_dim(tag_factors, tag_offset, tag_share.shape[0], 0),
            tag_share,
            step_tags,
        )
        new_users, new_tags = doubling_gather(
            [fresh_users, fresh_tags], "loop", loop_count, loop_position
        )
    item_part = transposed_product(rating_errors, user_factors) + jnp.dot(
        link_errors, tag_factors, preferred_element_type=jnp.float32
    )
    if got is not None:
        item_part, _ = lax.optimization_barrier((item_part, got))
    group_stages = radix_stages(group_count)
    item_share, item_offset = radix_scatter(
        item_part, "group", group_count, group_position, group_stages
    )
    fresh_items = advance(
        lax.dynamic_slice_in_dim(item_factors, item_offset, item_share.shape[0], 0),
        item_share,
        step_items,
    )
    new_items = radix_gather(fresh_items, "group", group_count, group_position, group_stages)
    return (new_users, new_items, new_tags)


def solution(mesh):
    in_specs = (
        P("group", None),
        P("loop", None),
        P("group", None),
        P("group", "loop"),
        P("group", "loop"),
        P("loop", "group"),
        P("loop", "group"),
    )
    out_specs = (P("group", None), P("loop", None), P("group", None))
    return jax.shard_map(shards, mesh=mesh, in_specs=in_specs, out_specs=out_specs, check_vma=False)
```

```python
import jax
import jax.numpy as jnp
from jax import lax
from jax.sharding import PartitionSpec as P

step_users = 0.015
step_items = 0.004
step_tags = 0.015


def tile_masked(values, tile_flags):
    height, breadth = values.shape
    blocks = values.reshape(height // 128, 128, breadth // 128, 128)
    masked = blocks * tile_flags.astype(jnp.float32)[:, None, :, None]
    return masked.reshape(height, breadth)


def residual_of(observed, row_factors, column_factors, tile_flags):
    predicted = lax.dot_general(
        row_factors, column_factors, (((1,), (1,)), ((), ())), preferred_element_type=jnp.float32
    )
    return tile_masked(observed.astype(jnp.float32) - predicted, tile_flags).astype(jnp.bfloat16)


def transposed_product(first_operand, second_operand):
    return lax.dot_general(
        first_operand, second_operand, (((0,), (0,)), ((), ())), preferred_element_type=jnp.float32
    )


def advance(factors, gradient, rate):
    return (factors.astype(jnp.float32) + rate * gradient).astype(jnp.bfloat16)


def xor_pairs(count, bit, mask=0):
    mask = mask or (1 << bit)
    return [(i, i ^ mask) for i in range(count)]


def halving_scatter(parts, axis, count, position):
    steps = count.bit_length() - 1
    offsets = [0 for _ in parts]
    for bit in range(steps):
        side = (position >> bit) & 1
        halves = [p.shape[0] // 2 for p in parts]
        kept = [lax.dynamic_slice_in_dim(p, side * h, h, 0) for p, h in zip(parts, halves)]
        sent = [lax.dynamic_slice_in_dim(p, (1 - side) * h, h, 0) for p, h in zip(parts, halves)]
        got = lax.ppermute(tuple(sent), axis, xor_pairs(count, bit))
        parts = [k + g for k, g in zip(kept, got)]
        offsets = [o + side * h for o, h in zip(offsets, halves)]
    return parts, offsets


def doubling_gather(parts, axis, count, position):
    steps = count.bit_length() - 1
    for bit in reversed(range(steps)):
        side = (position >> bit) & 1
        got = lax.ppermute(tuple(parts), axis, xor_pairs(count, bit))
        parts = [
            jnp.where(side == 0, jnp.concatenate([m, g], 0), jnp.concatenate([g, m], 0))
            for m, g in zip(parts, got)
        ]
    return parts


def radix_stages(count):
    bits = count.bit_length() - 1
    stages = []
    low = 0
    while low < bits:
        width = 1 if low == 0 else min(3, bits - low)
        stages.append((low, width))
        low += width
    return stages


def radix_scatter(part, axis, count, position, stages):
    offset = 0
    for low, width in stages:
        radix = 1 << width
        local = (position >> low) & (radix - 1)
        rows = part.shape[0] // radix
        total = lax.dynamic_slice_in_dim(part, local * rows, rows, 0)
        for shift in range(1, radix):
            sent = lax.dynamic_slice_in_dim(part, (local ^ shift) * rows, rows, 0)
            total = total + lax.ppermute(sent, axis, xor_pairs(count, 0, shift << low))
        part = total
        offset = offset + local * rows
    return part, offset


def radix_gather(share, axis, count, position, stages):
    for low, width in reversed(stages):
        radix = 1 << width
        local = (position >> low) & (radix - 1)
        pieces = [share] + [
            lax.ppermute(share, axis, xor_pairs(count, 0, shift << low))
            for shift in range(1, radix)
        ]
        stacked = jnp.stack(pieces, 0)
        share = jnp.concatenate(
            [lax.dynamic_index_in_dim(stacked, local ^ block, 0, False) for block in range(radix)],
            0,
        )
    return share


def loop_pair_step(user_factors, item_factors, tag_factors, rating_errors, link_errors, position):
    user_half = user_factors.shape[0] // 2
    tag_half = tag_factors.shape[0] // 2
    side = position & 1

    def partial(rows_side):
        users = jnp.dot(
            lax.dynamic_slice_in_dim(rating_errors, rows_side * user_half, user_half, 0),
            item_factors,
            preferred_element_type=jnp.float32,
        )
        tags = transposed_product(
            lax.dynamic_slice_in_dim(link_errors, rows_side * tag_half, tag_half, 1),
            item_factors,
        )
        return jnp.concatenate([users, tags], 0)

    sent = partial(1 - side)
    sent, rating_errors, link_errors = lax.optimization_barrier((sent, rating_errors, link_errors))
    got = lax.ppermute(sent, "loop", [(0, 1), (1, 0)])
    total = partial(side) + got
    fresh = jnp.concatenate(
        [
            advance(
                lax.dynamic_slice_in_dim(user_factors, side * user_half, user_half, 0),
                total[:user_half],
                step_users,
            ),
            advance(
                lax.dynamic_slice_in_dim(tag_factors, side * tag_half, tag_half, 0),
                total[user_half:],
                step_tags,
            ),
        ],
        0,
    )
    other = lax.ppermute(fresh, "loop", [(0, 1), (1, 0)])
    low = jnp.where(side == 0, fresh, other)
    high = jnp.where(side == 0, other, fresh)
    new_users = jnp.concatenate([low[:user_half], high[:user_half]], 0)
    new_tags = jnp.concatenate([low[user_half:], high[user_half:]], 0)
    return new_users, new_tags, rating_errors, link_errors, got


def shards(user_factors, item_factors, tag_factors, ratings, rating_tiles, tag_links, link_tiles):
    group_count = lax.axis_size("group")
    loop_count = lax.axis_size("loop")
    group_position = lax.axis_index("group")
    loop_position = lax.axis_index("loop")

    link_errors = residual_of(tag_links, item_factors, tag_factors, link_tiles)
    rating_errors = residual_of(ratings, user_factors, item_factors, rating_tiles)
    if loop_count == 2:
        new_users, new_tags, rating_errors, link_errors, got = loop_pair_step(
            user_factors, item_factors, tag_factors, rating_errors, link_errors, loop_position
        )
    else:
        got = None
        user_part = jnp.dot(rating_errors, item_factors, preferred_element_type=jnp.float32)
        tag_part = transposed_product(link_errors, item_factors)
        (user_share, tag_share), (user_offset, tag_offset) = halving_scatter(
            [user_part, tag_part], "loop", loop_count, loop_position
        )
        fresh_users = advance(
            lax.dynamic_slice_in_dim(user_factors, user_offset, user_share.shape[0], 0),
            user_share,
            step_users,
        )
        fresh_tags = advance(
            lax.dynamic_slice_in_dim(tag_factors, tag_offset, tag_share.shape[0], 0),
            tag_share,
            step_tags,
        )
        new_users, new_tags = doubling_gather(
            [fresh_users, fresh_tags], "loop", loop_count, loop_position
        )
    item_part = transposed_product(rating_errors, user_factors) + jnp.dot(
        link_errors, tag_factors, preferred_element_type=jnp.float32
    )
    (item_share,), (item_offset,) = halving_scatter([item_part], "group", group_count, group_position)
    if got is not None:
        item_share, _ = lax.optimization_barrier((item_share, got))
    fresh_items = advance(
        lax.dynamic_slice_in_dim(item_factors, item_offset, item_share.shape[0], 0),
        item_share,
        step_items,
    )
    (new_items,) = doubling_gather([fresh_items], "group", group_count, group_position)
    return (new_users, new_items, new_tags)


def solution(mesh):
    in_specs = (
        P("group", None),
        P("loop", None),
        P("group", None),
        P("group", "loop"),
        P("group", "loop"),
        P("loop", "group"),
        P("loop", "group"),
    )
    out_specs = (P("group", None), P("loop", None), P("group", None))
    return jax.shard_map(shards, mesh=mesh, in_specs=in_specs, out_specs=out_specs, check_vma=False)
```

```python
import jax
import jax.numpy as jnp
from jax import lax
from jax.sharding import PartitionSpec as P

step_users = 0.015
step_items = 0.004
step_tags = 0.015


def tile_masked(values, tile_flags):
    height, breadth = values.shape
    blocks = values.reshape(height // 128, 128, breadth // 128, 128)
    masked = blocks * tile_flags.astype(jnp.float32)[:, None, :, None]
    return masked.reshape(height, breadth)


def residual_of(observed, row_factors, column_factors, tile_flags):
    predicted = lax.dot_general(
        row_factors, column_factors, (((1,), (1,)), ((), ())), preferred_element_type=jnp.float32
    )
    return tile_masked(observed.astype(jnp.float32) - predicted, tile_flags).astype(jnp.bfloat16)


def transposed_product(first_operand, second_operand):
    return lax.dot_general(
        first_operand, second_operand, (((0,), (0,)), ((), ())), preferred_element_type=jnp.float32
    )


def advance(factors, gradient, rate):
    return (factors.astype(jnp.float32) + rate * gradient).astype(jnp.bfloat16)


def xor_pairs(count, bit):
    return [(i, i ^ (1 << bit)) for i in range(count)]


def halving_scatter(parts, axis, count, position):
    steps = count.bit_length() - 1
    offsets = [0 for _ in parts]
    for bit in range(steps):
        side = (position >> bit) & 1
        halves = [p.shape[0] // 2 for p in parts]
        kept = [lax.dynamic_slice_in_dim(p, side * h, h, 0) for p, h in zip(parts, halves)]
        sent = [lax.dynamic_slice_in_dim(p, (1 - side) * h, h, 0) for p, h in zip(parts, halves)]
        got = lax.ppermute(tuple(sent), axis, xor_pairs(count, bit))
        parts = [k + g for k, g in zip(kept, got)]
        offsets = [o + side * h for o, h in zip(offsets, halves)]
    return parts, offsets


def doubling_gather(parts, axis, count, position, tie=None, tie_step=-1):
    steps = count.bit_length() - 1
    for bit in reversed(range(steps)):
        if bit == tie_step and tie is not None:
            parts, _ = lax.optimization_barrier((parts, tie))
        side = (position >> bit) & 1
        got = lax.ppermute(tuple(parts), axis, xor_pairs(count, bit))
        parts = [
            jnp.where(side == 0, jnp.concatenate([m, g], 0), jnp.concatenate([g, m], 0))
            for m, g in zip(parts, got)
        ]
    return parts


def shards(user_factors, item_factors, tag_factors, ratings, rating_tiles, tag_links, link_tiles):
    group_count = lax.axis_size("group")
    loop_count = lax.axis_size("loop")
    group_position = lax.axis_index("group")
    loop_position = lax.axis_index("loop")

    link_errors = residual_of(tag_links, item_factors, tag_factors, link_tiles)
    rating_errors = residual_of(ratings, user_factors, item_factors, rating_tiles)
    user_part = jnp.dot(rating_errors, item_factors, preferred_element_type=jnp.float32)
    tag_part = transposed_product(link_errors, item_factors)
    joint_part = jnp.concatenate([user_part, tag_part], 0)

    joint_part, rating_errors, link_errors = lax.optimization_barrier(
        (joint_part, rating_errors, link_errors)
    )
    (joint_share,), (joint_offset,) = halving_scatter(
        [joint_part], "loop", loop_count, loop_position
    )
    item_part = transposed_product(rating_errors, user_factors) + jnp.dot(
        link_errors, tag_factors, preferred_element_type=jnp.float32
    )
    joint_factors = jnp.concatenate([user_factors, tag_factors], 0)
    fresh_joint = advance(
        lax.dynamic_slice_in_dim(joint_factors, joint_offset, joint_share.shape[0], 0),
        joint_share,
        jnp.where(
            joint_offset + jnp.arange(joint_share.shape[0])[:, None] < user_factors.shape[0],
            step_users,
            step_tags,
        ),
    )
    (new_joint,) = doubling_gather([fresh_joint], "loop", loop_count, loop_position)
    new_users = new_joint[: user_factors.shape[0]]
    new_tags = new_joint[user_factors.shape[0] :]

    (item_share,), (item_offset,) = halving_scatter([item_part], "group", group_count, group_position)
    fresh_items = advance(
        lax.dynamic_slice_in_dim(item_factors, item_offset, item_share.shape[0], 0),
        item_share,
        step_items,
    )
    (new_items,) = doubling_gather(
        [fresh_items], "group", group_count, group_position, new_joint, 1
    )
    return (new_users, new_items, new_tags)


def solution(mesh):
    in_specs = (
        P("group", None),
        P("loop", None),
        P("group", None),
        P("group", "loop"),
        P("group", "loop"),
        P("loop", "group"),
        P("loop", "group"),
    )
    out_specs = (P("group", None), P("loop", None), P("group", None))
    return jax.shard_map(shards, mesh=mesh, in_specs=in_specs, out_specs=out_specs, check_vma=False)
```

```python
import jax
import jax.numpy as jnp
from jax import lax
from jax.sharding import PartitionSpec as P

step_users = 0.015
step_items = 0.004
step_tags = 0.015


def tile_masked(values, tile_flags):
    height, breadth = values.shape
    blocks = values.reshape(height // 128, 128, breadth // 128, 128)
    masked = blocks * tile_flags.astype(jnp.float32)[:, None, :, None]
    return masked.reshape(height, breadth)


def residual_of(observed, row_factors, column_factors, tile_flags):
    predicted = lax.dot_general(
        row_factors, column_factors, (((1,), (1,)), ((), ())), preferred_element_type=jnp.float32
    )
    return tile_masked(observed.astype(jnp.float32) - predicted, tile_flags).astype(jnp.bfloat16)


def transposed_product(first_operand, second_operand):
    return lax.dot_general(
        first_operand, second_operand, (((0,), (0,)), ((), ())), preferred_element_type=jnp.float32
    )


def advance(factors, gradient, rate):
    return (factors.astype(jnp.float32) + rate * gradient).astype(jnp.bfloat16)


def xor_pairs(count, bit):
    return [(i, i ^ (1 << bit)) for i in range(count)]


def halving_scatter(parts, axis, count, position, tie=None, tie_step=-1):
    steps = count.bit_length() - 1
    offsets = [0 for _ in parts]
    for bit in range(steps):
        if bit == tie_step and tie is not None:
            parts, _ = lax.optimization_barrier((parts, tie))
        side = (position >> bit) & 1
        halves = [p.shape[0] // 2 for p in parts]
        kept = [lax.dynamic_slice_in_dim(p, side * h, h, 0) for p, h in zip(parts, halves)]
        sent = [lax.dynamic_slice_in_dim(p, (1 - side) * h, h, 0) for p, h in zip(parts, halves)]
        got = lax.ppermute(tuple(sent), axis, xor_pairs(count, bit))
        parts = [k + g for k, g in zip(kept, got)]
        offsets = [o + side * h for o, h in zip(offsets, halves)]
    return parts, offsets


def doubling_gather(parts, axis, count, position):
    steps = count.bit_length() - 1
    for bit in reversed(range(steps)):
        side = (position >> bit) & 1
        got = lax.ppermute(tuple(parts), axis, xor_pairs(count, bit))
        parts = [
            jnp.where(side == 0, jnp.concatenate([m, g], 0), jnp.concatenate([g, m], 0))
            for m, g in zip(parts, got)
        ]
    return parts


def shards(user_factors, item_factors, tag_factors, ratings, rating_tiles, tag_links, link_tiles):
    group_count = lax.axis_size("group")
    loop_count = lax.axis_size("loop")
    group_position = lax.axis_index("group")
    loop_position = lax.axis_index("loop")

    link_errors = residual_of(tag_links, item_factors, tag_factors, link_tiles)
    rating_errors = residual_of(ratings, user_factors, item_factors, rating_tiles)
    user_part = jnp.dot(rating_errors, item_factors, preferred_element_type=jnp.float32)
    tag_part = transposed_product(link_errors, item_factors)
    joint_part = jnp.concatenate([user_part, tag_part], 0)

    joint_part, rating_errors, link_errors = lax.optimization_barrier(
        (joint_part, rating_errors, link_errors)
    )
    (joint_share,), (joint_offset,) = halving_scatter(
        [joint_part], "loop", loop_count, loop_position
    )
    item_part = transposed_product(rating_errors, user_factors) + jnp.dot(
        link_errors, tag_factors, preferred_element_type=jnp.float32
    )
    joint_factors = jnp.concatenate([user_factors, tag_factors], 0)
    fresh_joint = advance(
        lax.dynamic_slice_in_dim(joint_factors, joint_offset, joint_share.shape[0], 0),
        joint_share,
        jnp.where(
            joint_offset + jnp.arange(joint_share.shape[0])[:, None] < user_factors.shape[0],
            step_users,
            step_tags,
        ),
    )
    (new_joint,) = doubling_gather([fresh_joint], "loop", loop_count, loop_position)
    new_users = new_joint[: user_factors.shape[0]]
    new_tags = new_joint[user_factors.shape[0] :]

    (item_share,), (item_offset,) = halving_scatter(
        [item_part], "group", group_count, group_position, joint_share, 3
    )
    fresh_items = advance(
        lax.dynamic_slice_in_dim(item_factors, item_offset, item_share.shape[0], 0),
        item_share,
        step_items,
    )
    (new_items,) = doubling_gather([fresh_items], "group", group_count, group_position)
    return (new_users, new_items, new_tags)


def solution(mesh):
    in_specs = (
        P("group", None),
        P("loop", None),
        P("group", None),
        P("group", "loop"),
        P("group", "loop"),
        P("loop", "group"),
        P("loop", "group"),
    )
    out_specs = (P("group", None), P("loop", None), P("group", None))
    return jax.shard_map(shards, mesh=mesh, in_specs=in_specs, out_specs=out_specs, check_vma=False)
```

```python
import jax
import jax.numpy as jnp
from jax import lax
from jax.sharding import PartitionSpec as P

step_users = 0.015
step_items = 0.004
step_tags = 0.015


def tile_masked(values, tile_flags):
    height, breadth = values.shape
    blocks = values.reshape(height // 128, 128, breadth // 128, 128)
    masked = blocks * tile_flags.astype(jnp.float32)[:, None, :, None]
    return masked.reshape(height, breadth)


def residual_of(observed, row_factors, column_factors, tile_flags):
    predicted = lax.dot_general(
        row_factors, column_factors, (((1,), (1,)), ((), ())), preferred_element_type=jnp.float32
    )
    return tile_masked(observed.astype(jnp.float32) - predicted, tile_flags).astype(jnp.bfloat16)


def transposed_product(first_operand, second_operand):
    return lax.dot_general(
        first_operand, second_operand, (((0,), (0,)), ((), ())), preferred_element_type=jnp.float32
    )


def advance(factors, gradient, rate):
    return (factors.astype(jnp.float32) + rate * gradient).astype(jnp.bfloat16)


def xor_pairs(count, bit):
    return [(i, i ^ (1 << bit)) for i in range(count)]


def halving_scatter(parts, axis, count, position, tie=None):
    steps = count.bit_length() - 1
    offsets = [0 for _ in parts]
    for bit in range(steps):
        side = (position >> bit) & 1
        halves = [p.shape[0] // 2 for p in parts]
        kept = [lax.dynamic_slice_in_dim(p, side * h, h, 0) for p, h in zip(parts, halves)]
        sent = [lax.dynamic_slice_in_dim(p, (1 - side) * h, h, 0) for p, h in zip(parts, halves)]
        got = lax.ppermute(tuple(sent), axis, xor_pairs(count, bit))
        if tie is not None:
            got, tie = lax.optimization_barrier((got, tie))
        parts = [k + g for k, g in zip(kept, got)]
        offsets = [o + side * h for o, h in zip(offsets, halves)]
    if tie is not None:
        return parts, offsets, tie
    return parts, offsets


def doubling_gather(parts, axis, count, position, bits=None):
    steps = count.bit_length() - 1
    for bit in reversed(range(steps)) if bits is None else bits:
        side = (position >> bit) & 1
        got = lax.ppermute(tuple(parts), axis, xor_pairs(count, bit))
        parts = [
            jnp.where(side == 0, jnp.concatenate([m, g], 0), jnp.concatenate([g, m], 0))
            for m, g in zip(parts, got)
        ]
    return parts


def shards(user_factors, item_factors, tag_factors, ratings, rating_tiles, tag_links, link_tiles):
    group_count = lax.axis_size("group")
    loop_count = lax.axis_size("loop")
    group_position = lax.axis_index("group")
    loop_position = lax.axis_index("loop")

    link_errors = residual_of(tag_links, item_factors, tag_factors, link_tiles)
    rating_errors = residual_of(ratings, user_factors, item_factors, rating_tiles)
    user_part = jnp.dot(rating_errors, item_factors, preferred_element_type=jnp.float32)
    tag_part = transposed_product(link_errors, item_factors)
    joint_part = jnp.concatenate([user_part, tag_part], 0)

    item_part = transposed_product(rating_errors, user_factors) + jnp.dot(
        link_errors, tag_factors, preferred_element_type=jnp.float32
    )
    group_steps = group_count.bit_length() - 1
    late_bits = [bit for bit in (1, 0) if bit < group_steps]
    early_bits = [bit for bit in reversed(range(group_steps)) if bit not in late_bits]
    always = group_position >= 0

    def group_early(item_part, item_factors):
        (item_share,), (item_offset,) = halving_scatter(
            [item_part], "group", group_count, group_position
        )
        fresh_items = advance(
            lax.dynamic_slice_in_dim(item_factors, item_offset, item_share.shape[0], 0),
            item_share,
            step_items,
        )
        (partly,) = doubling_gather(
            [fresh_items], "group", group_count, group_position, early_bits
        )
        return partly

    partly_rows = item_factors.shape[0] >> len(late_bits)
    partly = lax.cond(
        always,
        group_early,
        lambda p, f: jnp.zeros((partly_rows, f.shape[1]), jnp.bfloat16),
        item_part,
        item_factors,
    )
    (joint_share,), (joint_offset,), partly = halving_scatter(
        [joint_part], "loop", loop_count, loop_position, partly
    )
    joint_factors = jnp.concatenate([user_factors, tag_factors], 0)
    fresh_joint = advance(
        lax.dynamic_slice_in_dim(joint_factors, joint_offset, joint_share.shape[0], 0),
        joint_share,
        jnp.where(
            joint_offset + jnp.arange(joint_share.shape[0])[:, None] < user_factors.shape[0],
            step_users,
            step_tags,
        ),
    )
    (new_joint,) = doubling_gather([fresh_joint], "loop", loop_count, loop_position)
    new_users = new_joint[: user_factors.shape[0]]
    new_tags = new_joint[user_factors.shape[0] :]

    partly, _ = lax.optimization_barrier((partly, fresh_joint))

    def group_late(partly):
        (whole,) = doubling_gather([partly], "group", group_count, group_position, late_bits)
        return whole

    new_items = lax.cond(
        always,
        group_late,
        lambda p: jnp.zeros(item_factors.shape, jnp.bfloat16),
        partly,
    )
    return (new_users, new_items, new_tags)


def solution(mesh):
    in_specs = (
        P("group", None),
        P("loop", None),
        P("group", None),
        P("group", "loop"),
        P("group", "loop"),
        P("loop", "group"),
        P("loop", "group"),
    )
    out_specs = (P("group", None), P("loop", None), P("group", None))
    return jax.shard_map(shards, mesh=mesh, in_specs=in_specs, out_specs=out_specs, check_vma=False)
```

```python
import jax
import jax.numpy as jnp
from jax import lax
from jax.experimental import pallas as pl
from jax.experimental.pallas import tpu as pltpu
from jax.sharding import PartitionSpec as P

step_users = 0.015
step_items = 0.004
step_tags = 0.015


def tile_masked(values, tile_flags):
    height, breadth = values.shape
    blocks = values.reshape(height // 128, 128, breadth // 128, 128)
    masked = blocks * tile_flags.astype(jnp.float32)[:, None, :, None]
    return masked.reshape(height, breadth)


def residual_of(observed, row_factors, column_factors, tile_flags):
    predicted = lax.dot_general(
        row_factors, column_factors, (((1,), (1,)), ((), ())), preferred_element_type=jnp.float32
    )
    return tile_masked(observed.astype(jnp.float32) - predicted, tile_flags).astype(jnp.bfloat16)


def transposed_product(first_operand, second_operand):
    return lax.dot_general(
        first_operand, second_operand, (((0,), (0,)), ((), ())), preferred_element_type=jnp.float32
    )


def advance(factors, gradient, rate):
    return (factors.astype(jnp.float32) + rate * gradient).astype(jnp.bfloat16)


def xor_pairs(count, bit):
    return [(i, i ^ (1 << bit)) for i in range(count)]


def halving_scatter(parts, axis, count, position):
    steps = count.bit_length() - 1
    offsets = [0 for _ in parts]
    for bit in range(steps):
        side = (position >> bit) & 1
        halves = [p.shape[0] // 2 for p in parts]
        kept = [lax.dynamic_slice_in_dim(p, side * h, h, 0) for p, h in zip(parts, halves)]
        sent = [lax.dynamic_slice_in_dim(p, (1 - side) * h, h, 0) for p, h in zip(parts, halves)]
        got = lax.ppermute(tuple(sent), axis, xor_pairs(count, bit))
        parts = [k + g for k, g in zip(kept, got)]
        offsets = [o + side * h for o, h in zip(offsets, halves)]
    return parts, offsets


def doubling_gather(parts, axis, count, position):
    steps = count.bit_length() - 1
    for bit in reversed(range(steps)):
        side = (position >> bit) & 1
        got = lax.ppermute(tuple(parts), axis, xor_pairs(count, bit))
        parts = [
            jnp.where(side == 0, jnp.concatenate([m, g], 0), jnp.concatenate([g, m], 0))
            for m, g in zip(parts, got)
        ]
    return parts


def rating_kernel(flags_ref, u_ref, i_ref, r_ref, user_ref, item_ref):
    block = pl.program_id(0)
    users = u_ref[...]
    items = i_ref[...]
    predicted = lax.dot_general(users, items, (((1,), (1,)), ((), ())), preferred_element_type=jnp.float32)
    residual = r_ref[...].astype(jnp.float32) - predicted
    column_tile = lax.broadcasted_iota(jnp.int32, (1, residual.shape[1]), 1) // 128
    mask = jnp.zeros((1, residual.shape[1]), jnp.float32)
    for tile in range(residual.shape[1] // 128):
        mask = jnp.where(column_tile == tile, flags_ref[block, tile].astype(jnp.float32), mask)
    errors = (residual * mask).astype(jnp.bfloat16)
    user_ref[...] = jnp.dot(errors, items, preferred_element_type=jnp.float32)

    @pl.when(block == 0)
    def _():
        item_ref[...] = jnp.zeros_like(item_ref)

    item_ref[...] += lax.dot_general(errors, users, (((0,), (0,)), ((), ())), preferred_element_type=jnp.float32)


def rating_partials(user_factors, item_factors, ratings, rating_tiles):
    rows, rank = user_factors.shape
    cols = item_factors.shape[0]
    return pl.pallas_call(
        rating_kernel,
        grid_spec=pltpu.PrefetchScalarGridSpec(
            num_scalar_prefetch=1,
            grid=(rows // 128,),
            in_specs=[
                pl.BlockSpec((128, rank), lambda b, f: (b, 0)),
                pl.BlockSpec((cols, rank), lambda b, f: (0, 0)),
                pl.BlockSpec((128, cols), lambda b, f: (b, 0)),
            ],
            out_specs=[
                pl.BlockSpec((128, rank), lambda b, f: (b, 0)),
                pl.BlockSpec((cols, rank), lambda b, f: (0, 0)),
            ],
        ),
        out_shape=[
            jax.ShapeDtypeStruct((rows, rank), jnp.float32),
            jax.ShapeDtypeStruct((cols, rank), jnp.float32),
        ],
        compiler_params=pltpu.CompilerParams(dimension_semantics=("arbitrary",)),
    )(rating_tiles, user_factors, item_factors, ratings)


def shards(user_factors, item_factors, tag_factors, ratings, rating_tiles, tag_links, link_tiles):
    group_count = lax.axis_size("group")
    loop_count = lax.axis_size("loop")
    group_position = lax.axis_index("group")
    loop_position = lax.axis_index("loop")

    link_errors = residual_of(tag_links, item_factors, tag_factors, link_tiles)
    user_part, rating_item_part = rating_partials(
        user_factors, item_factors, ratings, rating_tiles
    )
    tag_part = transposed_product(link_errors, item_factors)
    joint_part = jnp.concatenate([user_part, tag_part], 0)
    item_part = rating_item_part + jnp.dot(
        link_errors, tag_factors, preferred_element_type=jnp.float32
    )
    (joint_share,), (joint_offset,) = halving_scatter(
        [joint_part], "loop", loop_count, loop_position
    )
    joint_factors = jnp.concatenate([user_factors, tag_factors], 0)
    fresh_joint = advance(
        lax.dynamic_slice_in_dim(joint_factors, joint_offset, joint_share.shape[0], 0),
        joint_share,
        jnp.where(
            joint_offset + jnp.arange(joint_share.shape[0])[:, None] < user_factors.shape[0],
            step_users,
            step_tags,
        ),
    )
    (new_joint,) = doubling_gather([fresh_joint], "loop", loop_count, loop_position)
    new_users = new_joint[: user_factors.shape[0]]
    new_tags = new_joint[user_factors.shape[0] :]

    (item_share,), (item_offset,) = halving_scatter([item_part], "group", group_count, group_position)
    fresh_items = advance(
        lax.dynamic_slice_in_dim(item_factors, item_offset, item_share.shape[0], 0),
        item_share,
        step_items,
    )
    (new_items,) = doubling_gather([fresh_items], "group", group_count, group_position)
    return (new_users, new_items, new_tags)


def solution(mesh):
    in_specs = (
        P("group", None),
        P("loop", None),
        P("group", None),
        P("group", "loop"),
        P("group", "loop"),
        P("loop", "group"),
        P("loop", "group"),
    )
    out_specs = (P("group", None), P("loop", None), P("group", None))
    return jax.shard_map(shards, mesh=mesh, in_specs=in_specs, out_specs=out_specs, check_vma=False)
```

```python
import jax
import jax.numpy as jnp
from jax import lax
from jax.experimental import pallas as pl
from jax.experimental.pallas import tpu as pltpu
from jax.sharding import PartitionSpec as P

step_users = 0.015
step_items = 0.004
step_tags = 0.015


def tile_masked(values, tile_flags):
    height, breadth = values.shape
    blocks = values.reshape(height // 128, 128, breadth // 128, 128)
    masked = blocks * tile_flags.astype(jnp.float32)[:, None, :, None]
    return masked.reshape(height, breadth)


def residual_of(observed, row_factors, column_factors, tile_flags):
    predicted = lax.dot_general(
        row_factors, column_factors, (((1,), (1,)), ((), ())), preferred_element_type=jnp.float32
    )
    return tile_masked(observed.astype(jnp.float32) - predicted, tile_flags).astype(jnp.bfloat16)


def transposed_product(first_operand, second_operand):
    return lax.dot_general(
        first_operand, second_operand, (((0,), (0,)), ((), ())), preferred_element_type=jnp.float32
    )


def advance(factors, gradient, rate):
    return (factors.astype(jnp.float32) + rate * gradient).astype(jnp.bfloat16)


def xor_pairs(count, bit):
    return [(i, i ^ (1 << bit)) for i in range(count)]


def halving_scatter(parts, axis, count, position):
    steps = count.bit_length() - 1
    offsets = [0 for _ in parts]
    for bit in range(steps):
        side = (position >> bit) & 1
        halves = [p.shape[0] // 2 for p in parts]
        kept = [lax.dynamic_slice_in_dim(p, side * h, h, 0) for p, h in zip(parts, halves)]
        sent = [lax.dynamic_slice_in_dim(p, (1 - side) * h, h, 0) for p, h in zip(parts, halves)]
        got = lax.ppermute(tuple(sent), axis, xor_pairs(count, bit))
        parts = [k + g for k, g in zip(kept, got)]
        offsets = [o + side * h for o, h in zip(offsets, halves)]
    return parts, offsets


def doubling_gather(parts, axis, count, position):
    steps = count.bit_length() - 1
    for bit in reversed(range(steps)):
        side = (position >> bit) & 1
        got = lax.ppermute(tuple(parts), axis, xor_pairs(count, bit))
        parts = [
            jnp.where(side == 0, jnp.concatenate([m, g], 0), jnp.concatenate([g, m], 0))
            for m, g in zip(parts, got)
        ]
    return parts


def rating_kernel(flags_ref, u_ref, i_ref, r_ref, user_ref, item_ref, err_ref):
    block = pl.program_id(0)
    users = u_ref[...]
    items = i_ref[...]
    block_rows, cols = err_ref.shape
    predicted = lax.dot_general(users, items, (((1,), (1,)), ((), ())), preferred_element_type=jnp.float32)
    column_tile = lax.broadcasted_iota(jnp.int32, (1, cols), 1) // 128
    row_tiles = block_rows // 128
    for row_tile in range(row_tiles):
        rows = slice(row_tile * 128, (row_tile + 1) * 128)
        mask = jnp.zeros((1, cols), jnp.float32)
        for tile in range(cols // 128):
            flag = flags_ref[block * row_tiles + row_tile, tile].astype(jnp.float32)
            mask = jnp.where(column_tile == tile, flag, mask)
        residual = r_ref[rows, :].astype(jnp.float32) - predicted[rows, :]
        err_ref[rows, :] = (residual * mask).astype(jnp.bfloat16)
    errors = err_ref[...]
    user_ref[...] = jnp.dot(errors, items, preferred_element_type=jnp.float32)

    @pl.when(block == 0)
    def _():
        item_ref[...] = jnp.zeros_like(item_ref)

    item_ref[...] += lax.dot_general(errors, users, (((0,), (0,)), ((), ())), preferred_element_type=jnp.float32)


def rating_partials(user_factors, item_factors, ratings, rating_tiles):
    rows, rank = user_factors.shape
    cols = item_factors.shape[0]
    block_rows = 512 if rows % 512 == 0 else 128
    return pl.pallas_call(
        rating_kernel,
        grid_spec=pltpu.PrefetchScalarGridSpec(
            num_scalar_prefetch=1,
            grid=(rows // block_rows,),
            in_specs=[
                pl.BlockSpec((block_rows, rank), lambda b, f: (b, 0)),
                pl.BlockSpec((cols, rank), lambda b, f: (0, 0)),
                pl.BlockSpec((block_rows, cols), lambda b, f: (b, 0)),
            ],
            out_specs=[
                pl.BlockSpec((block_rows, rank), lambda b, f: (b, 0)),
                pl.BlockSpec((cols, rank), lambda b, f: (0, 0)),
            ],
            scratch_shapes=[pltpu.VMEM((block_rows, cols), jnp.bfloat16)],
        ),
        out_shape=[
            jax.ShapeDtypeStruct((rows, rank), jnp.float32),
            jax.ShapeDtypeStruct((cols, rank), jnp.float32),
        ],
        compiler_params=pltpu.CompilerParams(dimension_semantics=("arbitrary",)),
    )(rating_tiles, user_factors, item_factors, ratings)


def shards(user_factors, item_factors, tag_factors, ratings, rating_tiles, tag_links, link_tiles):
    group_count = lax.axis_size("group")
    loop_count = lax.axis_size("loop")
    group_position = lax.axis_index("group")
    loop_position = lax.axis_index("loop")

    link_errors = residual_of(tag_links, item_factors, tag_factors, link_tiles)
    user_part, rating_item_part = rating_partials(
        user_factors, item_factors, ratings, rating_tiles
    )
    tag_part = transposed_product(link_errors, item_factors)
    joint_part = jnp.concatenate([user_part, tag_part], 0)
    item_part = rating_item_part + jnp.dot(
        link_errors, tag_factors, preferred_element_type=jnp.float32
    )
    (joint_share,), (joint_offset,) = halving_scatter(
        [joint_part], "loop", loop_count, loop_position
    )
    joint_factors = jnp.concatenate([user_factors, tag_factors], 0)
    fresh_joint = advance(
        lax.dynamic_slice_in_dim(joint_factors, joint_offset, joint_share.shape[0], 0),
        joint_share,
        jnp.where(
            joint_offset + jnp.arange(joint_share.shape[0])[:, None] < user_factors.shape[0],
            step_users,
            step_tags,
        ),
    )
    (new_joint,) = doubling_gather([fresh_joint], "loop", loop_count, loop_position)
    new_users = new_joint[: user_factors.shape[0]]
    new_tags = new_joint[user_factors.shape[0] :]

    (item_share,), (item_offset,) = halving_scatter([item_part], "group", group_count, group_position)
    fresh_items = advance(
        lax.dynamic_slice_in_dim(item_factors, item_offset, item_share.shape[0], 0),
        item_share,
        step_items,
    )
    (new_items,) = doubling_gather([fresh_items], "group", group_count, group_position)
    return (new_users, new_items, new_tags)


def solution(mesh):
    in_specs = (
        P("group", None),
        P("loop", None),
        P("group", None),
        P("group", "loop"),
        P("group", "loop"),
        P("loop", "group"),
        P("loop", "group"),
    )
    out_specs = (P("group", None), P("loop", None), P("group", None))
    return jax.shard_map(shards, mesh=mesh, in_specs=in_specs, out_specs=out_specs, check_vma=False)
```

```python
import jax
import jax.numpy as jnp
from jax import lax
from jax.experimental import pallas as pl
from jax.experimental.pallas import tpu as pltpu
from jax.sharding import PartitionSpec as P

step_users = 0.015
step_items = 0.004
step_tags = 0.015


def tile_masked(values, tile_flags):
    height, breadth = values.shape
    blocks = values.reshape(height // 128, 128, breadth // 128, 128)
    masked = blocks * tile_flags.astype(jnp.float32)[:, None, :, None]
    return masked.reshape(height, breadth)


def residual_of(observed, row_factors, column_factors, tile_flags):
    predicted = lax.dot_general(
        row_factors, column_factors, (((1,), (1,)), ((), ())), preferred_element_type=jnp.float32
    )
    return tile_masked(observed.astype(jnp.float32) - predicted, tile_flags).astype(jnp.bfloat16)


def transposed_product(first_operand, second_operand):
    return lax.dot_general(
        first_operand, second_operand, (((0,), (0,)), ((), ())), preferred_element_type=jnp.float32
    )


def advance(factors, gradient, rate):
    return (factors.astype(jnp.float32) + rate * gradient).astype(jnp.bfloat16)


def xor_pairs(count, bit):
    return [(i, i ^ (1 << bit)) for i in range(count)]


def halving_scatter(parts, axis, count, position):
    steps = count.bit_length() - 1
    offsets = [0 for _ in parts]
    for bit in range(steps):
        side = (position >> bit) & 1
        halves = [p.shape[0] // 2 for p in parts]
        kept = [lax.dynamic_slice_in_dim(p, side * h, h, 0) for p, h in zip(parts, halves)]
        sent = [lax.dynamic_slice_in_dim(p, (1 - side) * h, h, 0) for p, h in zip(parts, halves)]
        got = lax.ppermute(tuple(sent), axis, xor_pairs(count, bit))
        parts = [k + g for k, g in zip(kept, got)]
        offsets = [o + side * h for o, h in zip(offsets, halves)]
    return parts, offsets


def doubling_gather(parts, axis, count, position):
    steps = count.bit_length() - 1
    for bit in reversed(range(steps)):
        side = (position >> bit) & 1
        got = lax.ppermute(tuple(parts), axis, xor_pairs(count, bit))
        parts = [
            jnp.where(side == 0, jnp.concatenate([m, g], 0), jnp.concatenate([g, m], 0))
            for m, g in zip(parts, got)
        ]
    return parts


def rating_kernel(flags_ref, u_ref, i_ref, r_ref, user_ref, item_ref, err_ref):
    block = pl.program_id(0)
    users = u_ref[...]
    items = i_ref[...]
    block_rows, cols = err_ref.shape
    predicted = lax.dot_general(users, items, (((1,), (1,)), ((), ())), preferred_element_type=jnp.float32)
    column_tile = lax.broadcasted_iota(jnp.int32, (1, cols), 1) // 128
    row_tiles = block_rows // 128
    for row_tile in range(row_tiles):
        rows = slice(row_tile * 128, (row_tile + 1) * 128)
        mask = jnp.zeros((1, cols), jnp.float32)
        for tile in range(cols // 128):
            flag = flags_ref[block * row_tiles + row_tile, tile].astype(jnp.float32)
            mask = jnp.where(column_tile == tile, flag, mask)
        residual = r_ref[rows, :].astype(jnp.float32) - predicted[rows, :]
        err_ref[rows, :] = (residual * mask).astype(jnp.bfloat16)
    errors = err_ref[...]
    user_ref[...] = jnp.dot(errors, items, preferred_element_type=jnp.float32)

    @pl.when(block == 0)
    def _():
        item_ref[...] = jnp.zeros_like(item_ref)

    item_ref[...] += lax.dot_general(users, errors, (((0,), (0,)), ((), ())), preferred_element_type=jnp.float32)


def rating_partials(user_factors, item_factors, ratings, rating_tiles):
    rows, rank = user_factors.shape
    cols = item_factors.shape[0]
    block_rows = 512 if rows % 512 == 0 else 128
    return pl.pallas_call(
        rating_kernel,
        grid_spec=pltpu.PrefetchScalarGridSpec(
            num_scalar_prefetch=1,
            grid=(rows // block_rows,),
            in_specs=[
                pl.BlockSpec((block_rows, rank), lambda b, f: (b, 0)),
                pl.BlockSpec((cols, rank), lambda b, f: (0, 0)),
                pl.BlockSpec((block_rows, cols), lambda b, f: (b, 0)),
            ],
            out_specs=[
                pl.BlockSpec((block_rows, rank), lambda b, f: (b, 0)),
                pl.BlockSpec((rank, cols), lambda b, f: (0, 0)),
            ],
            scratch_shapes=[pltpu.VMEM((block_rows, cols), jnp.bfloat16)],
        ),
        out_shape=[
            jax.ShapeDtypeStruct((rows, rank), jnp.float32),
            jax.ShapeDtypeStruct((rank, cols), jnp.float32),
        ],
        compiler_params=pltpu.CompilerParams(dimension_semantics=("arbitrary",)),
    )(rating_tiles, user_factors, item_factors, ratings)


def shards(user_factors, item_factors, tag_factors, ratings, rating_tiles, tag_links, link_tiles):
    group_count = lax.axis_size("group")
    loop_count = lax.axis_size("loop")
    group_position = lax.axis_index("group")
    loop_position = lax.axis_index("loop")

    link_errors = residual_of(tag_links, item_factors, tag_factors, link_tiles)
    user_part, rating_item_part = rating_partials(
        user_factors, item_factors, ratings, rating_tiles
    )
    tag_part = transposed_product(link_errors, item_factors)
    joint_part = jnp.concatenate([user_part, tag_part], 0)
    item_part = rating_item_part.T + jnp.dot(
        link_errors, tag_factors, preferred_element_type=jnp.float32
    )
    (joint_share,), (joint_offset,) = halving_scatter(
        [joint_part], "loop", loop_count, loop_position
    )
    joint_factors = jnp.concatenate([user_factors, tag_factors], 0)
    fresh_joint = advance(
        lax.dynamic_slice_in_dim(joint_factors, joint_offset, joint_share.shape[0], 0),
        joint_share,
        jnp.where(
            joint_offset + jnp.arange(joint_share.shape[0])[:, None] < user_factors.shape[0],
            step_users,
            step_tags,
        ),
    )
    (new_joint,) = doubling_gather([fresh_joint], "loop", loop_count, loop_position)
    new_users = new_joint[: user_factors.shape[0]]
    new_tags = new_joint[user_factors.shape[0] :]

    (item_share,), (item_offset,) = halving_scatter([item_part], "group", group_count, group_position)
    fresh_items = advance(
        lax.dynamic_slice_in_dim(item_factors, item_offset, item_share.shape[0], 0),
        item_share,
        step_items,
    )
    (new_items,) = doubling_gather([fresh_items], "group", group_count, group_position)
    return (new_users, new_items, new_tags)


def solution(mesh):
    in_specs = (
        P("group", None),
        P("loop", None),
        P("group", None),
        P("group", "loop"),
        P("group", "loop"),
        P("loop", "group"),
        P("loop", "group"),
    )
    out_specs = (P("group", None), P("loop", None), P("group", None))
    return jax.shard_map(shards, mesh=mesh, in_specs=in_specs, out_specs=out_specs, check_vma=False)
```

```python
import jax
import jax.numpy as jnp
from jax import lax
from jax.sharding import PartitionSpec as P

step_users = 0.015
step_items = 0.004
step_tags = 0.015


def tile_masked(values, tile_flags):
    height, breadth = values.shape
    blocks = values.reshape(height // 128, 128, breadth // 128, 128)
    masked = blocks * tile_flags.astype(jnp.float32)[:, None, :, None]
    return masked.reshape(height, breadth)


def residual_of(observed, row_factors, column_factors, tile_flags):
    predicted = lax.dot_general(
        row_factors, column_factors, (((1,), (1,)), ((), ())), preferred_element_type=jnp.float32
    )
    return tile_masked(observed.astype(jnp.float32) - predicted, tile_flags).astype(jnp.bfloat16)


def transposed_product(first_operand, second_operand):
    return lax.dot_general(
        first_operand, second_operand, (((0,), (0,)), ((), ())), preferred_element_type=jnp.float32
    )


def advance(factors, gradient, rate):
    return (factors.astype(jnp.float32) + rate * gradient).astype(jnp.bfloat16)


def xor_pairs(count, bit):
    return [(i, i ^ (1 << bit)) for i in range(count)]


def halving_scatter(parts, axis, count, position, bits=None):
    steps = count.bit_length() - 1
    offsets = [0 for _ in parts]
    for bit in range(steps) if bits is None else bits:
        side = (position >> bit) & 1
        halves = [p.shape[0] // 2 for p in parts]
        kept = [lax.dynamic_slice_in_dim(p, side * h, h, 0) for p, h in zip(parts, halves)]
        sent = [lax.dynamic_slice_in_dim(p, (1 - side) * h, h, 0) for p, h in zip(parts, halves)]
        got = lax.ppermute(tuple(sent), axis, xor_pairs(count, bit))
        parts = [k + g for k, g in zip(kept, got)]
        offsets = [o + side * h for o, h in zip(offsets, halves)]
    return parts, offsets


def doubling_gather(parts, axis, count, position):
    steps = count.bit_length() - 1
    for bit in reversed(range(steps)):
        side = (position >> bit) & 1
        got = lax.ppermute(tuple(parts), axis, xor_pairs(count, bit))
        parts = [
            jnp.where(side == 0, jnp.concatenate([m, g], 0), jnp.concatenate([g, m], 0))
            for m, g in zip(parts, got)
        ]
    return parts


def shards(user_factors, item_factors, tag_factors, ratings, rating_tiles, tag_links, link_tiles):
    group_count = lax.axis_size("group")
    loop_count = lax.axis_size("loop")
    group_position = lax.axis_index("group")
    loop_position = lax.axis_index("loop")

    link_errors = residual_of(tag_links, item_factors, tag_factors, link_tiles)
    rating_errors = residual_of(ratings, user_factors, item_factors, rating_tiles)
    user_part = jnp.dot(rating_errors, item_factors, preferred_element_type=jnp.float32)
    tag_part = transposed_product(link_errors, item_factors)
    joint_part = jnp.concatenate([user_part, tag_part], 0)

    joint_part, rating_errors, link_errors = lax.optimization_barrier(
        (joint_part, rating_errors, link_errors)
    )
    (joint_share,), (joint_offset,) = halving_scatter(
        [joint_part], "loop", loop_count, loop_position
    )
    item_part = transposed_product(rating_errors, user_factors) + jnp.dot(
        link_errors, tag_factors, preferred_element_type=jnp.float32
    )
    joint_factors = jnp.concatenate([user_factors, tag_factors], 0)
    fresh_joint = advance(
        lax.dynamic_slice_in_dim(joint_factors, joint_offset, joint_share.shape[0], 0),
        joint_share,
        jnp.where(
            joint_offset + jnp.arange(joint_share.shape[0])[:, None] < user_factors.shape[0],
            step_users,
            step_tags,
        ),
    )
    (new_joint,) = doubling_gather([fresh_joint], "loop", loop_count, loop_position)
    new_users = new_joint[: user_factors.shape[0]]
    new_tags = new_joint[user_factors.shape[0] :]

    group_steps = group_count.bit_length() - 1
    first_bits = list(range(min(2, group_steps)))
    first_rows = item_part.shape[0] >> len(first_bits)

    def group_first(item_part):
        (share,), (offset,) = halving_scatter(
            [item_part], "group", group_count, group_position, first_bits
        )
        return share, offset

    first_share, first_offset = lax.cond(
        group_position >= 0,
        group_first,
        lambda p: (jnp.zeros((first_rows, p.shape[1]), p.dtype), jnp.int32(0)),
        item_part,
    )
    (item_share,), (item_offset,) = halving_scatter(
        [first_share], "group", group_count, group_position, range(len(first_bits), group_steps)
    )
    item_offset = first_offset + item_offset
    fresh_items = advance(
        lax.dynamic_slice_in_dim(item_factors, item_offset, item_share.shape[0], 0),
        item_share,
        step_items,
    )
    (new_items,) = doubling_gather([fresh_items], "group", group_count, group_position)
    return (new_users, new_items, new_tags)


def solution(mesh):
    in_specs = (
        P("group", None),
        P("loop", None),
        P("group", None),
        P("group", "loop"),
        P("group", "loop"),
        P("loop", "group"),
        P("loop", "group"),
    )
    out_specs = (P("group", None), P("loop", None), P("group", None))
    return jax.shard_map(shards, mesh=mesh, in_specs=in_specs, out_specs=out_specs, check_vma=False)
```

```python
import jax
import jax.numpy as jnp
from jax import lax
from jax.sharding import PartitionSpec as P

step_users = 0.015
step_items = 0.004
step_tags = 0.015


def tile_masked(values, tile_flags):
    height, breadth = values.shape
    blocks = values.reshape(height // 128, 128, breadth // 128, 128)
    masked = blocks * tile_flags.astype(jnp.float32)[:, None, :, None]
    return masked.reshape(height, breadth)


def residual_of(observed, row_factors, column_factors, tile_flags):
    predicted = lax.dot_general(
        row_factors, column_factors, (((1,), (1,)), ((), ())), preferred_element_type=jnp.float32
    )
    return tile_masked(observed.astype(jnp.float32) - predicted, tile_flags).astype(jnp.bfloat16)


def transposed_product(first_operand, second_operand):
    return lax.dot_general(
        first_operand, second_operand, (((0,), (0,)), ((), ())), preferred_element_type=jnp.float32
    )


def advance(factors, gradient, rate):
    return (factors.astype(jnp.float32) + rate * gradient).astype(jnp.bfloat16)


def xor_pairs(count, bit):
    return [(i, i ^ (1 << bit)) for i in range(count)]


def halving_scatter(parts, axis, count, position, bits=None):
    steps = count.bit_length() - 1
    offsets = [0 for _ in parts]
    for bit in range(steps) if bits is None else bits:
        side = (position >> bit) & 1
        halves = [p.shape[0] // 2 for p in parts]
        kept = [lax.dynamic_slice_in_dim(p, side * h, h, 0) for p, h in zip(parts, halves)]
        sent = [lax.dynamic_slice_in_dim(p, (1 - side) * h, h, 0) for p, h in zip(parts, halves)]
        got = lax.ppermute(tuple(sent), axis, xor_pairs(count, bit))
        parts = [k + g for k, g in zip(kept, got)]
        offsets = [o + side * h for o, h in zip(offsets, halves)]
    return parts, offsets


def doubling_gather(parts, axis, count, position, bits=None):
    steps = count.bit_length() - 1
    for bit in reversed(range(steps)) if bits is None else bits:
        side = (position >> bit) & 1
        got = lax.ppermute(tuple(parts), axis, xor_pairs(count, bit))
        parts = [
            jnp.where(side == 0, jnp.concatenate([m, g], 0), jnp.concatenate([g, m], 0))
            for m, g in zip(parts, got)
        ]
    return parts


def shards(user_factors, item_factors, tag_factors, ratings, rating_tiles, tag_links, link_tiles):
    group_count = lax.axis_size("group")
    loop_count = lax.axis_size("loop")
    group_position = lax.axis_index("group")
    loop_position = lax.axis_index("loop")

    link_errors = residual_of(tag_links, item_factors, tag_factors, link_tiles)
    rating_errors = residual_of(ratings, user_factors, item_factors, rating_tiles)
    user_part = jnp.dot(rating_errors, item_factors, preferred_element_type=jnp.float32)
    tag_part = transposed_product(link_errors, item_factors)
    joint_part = jnp.concatenate([user_part, tag_part], 0)

    item_part = transposed_product(rating_errors, user_factors) + jnp.dot(
        link_errors, tag_factors, preferred_element_type=jnp.float32
    )
    joint_part, item_part = lax.optimization_barrier((joint_part, item_part))
    (joint_share,), (joint_offset,) = halving_scatter(
        [joint_part], "loop", loop_count, loop_position
    )
    group_steps = group_count.bit_length() - 1
    first_bits = list(range(min(2, group_steps)))
    first_rows = item_part.shape[0] >> len(first_bits)

    def group_first(item_part):
        (share,), (offset,) = halving_scatter(
            [item_part], "group", group_count, group_position, first_bits
        )
        return share, offset

    first_share, first_offset = lax.cond(
        group_position >= 0,
        group_first,
        lambda p: (jnp.zeros((first_rows, p.shape[1]), p.dtype), jnp.int32(0)),
        item_part,
    )
    (item_share,), (item_offset,) = halving_scatter(
        [first_share], "group", group_count, group_position, range(len(first_bits), group_steps)
    )
    item_offset = first_offset + item_offset
    fresh_items = advance(
        lax.dynamic_slice_in_dim(item_factors, item_offset, item_share.shape[0], 0),
        item_share,
        step_items,
    )
    gather_bits = list(reversed(range(group_steps)))
    (partly,) = doubling_gather(
        [fresh_items], "group", group_count, group_position, gather_bits[:1]
    )
    partly, joint_share = lax.optimization_barrier((partly, joint_share))
    joint_factors = jnp.concatenate([user_factors, tag_factors], 0)
    fresh_joint = advance(
        lax.dynamic_slice_in_dim(joint_factors, joint_offset, joint_share.shape[0], 0),
        joint_share,
        jnp.where(
            joint_offset + jnp.arange(joint_share.shape[0])[:, None] < user_factors.shape[0],
            step_users,
            step_tags,
        ),
    )
    (new_joint,) = doubling_gather([fresh_joint], "loop", loop_count, loop_position)
    new_users = new_joint[: user_factors.shape[0]]
    new_tags = new_joint[user_factors.shape[0] :]

    (partly,) = doubling_gather(
        [partly], "group", group_count, group_position, gather_bits[1:2]
    )
    partly, new_joint = lax.optimization_barrier((partly, new_joint))
    new_users = new_joint[: user_factors.shape[0]]
    new_tags = new_joint[user_factors.shape[0] :]
    (new_items,) = doubling_gather(
        [partly], "group", group_count, group_position, gather_bits[2:]
    )
    return (new_users, new_items, new_tags)


def solution(mesh):
    in_specs = (
        P("group", None),
        P("loop", None),
        P("group", None),
        P("group", "loop"),
        P("group", "loop"),
        P("loop", "group"),
        P("loop", "group"),
    )
    out_specs = (P("group", None), P("loop", None), P("group", None))
    return jax.shard_map(shards, mesh=mesh, in_specs=in_specs, out_specs=out_specs, check_vma=False)
```

```python
import jax
import jax.numpy as jnp
from jax import lax
from jax.sharding import PartitionSpec as P

step_users = 0.015
step_items = 0.004
step_tags = 0.015


def tile_masked(values, tile_flags):
    height, breadth = values.shape
    blocks = values.reshape(height // 128, 128, breadth // 128, 128)
    masked = blocks * tile_flags.astype(jnp.float32)[:, None, :, None]
    return masked.reshape(height, breadth)


def residual_of(observed, row_factors, column_factors, tile_flags):
    predicted = lax.dot_general(
        row_factors, column_factors, (((1,), (1,)), ((), ())), preferred_element_type=jnp.float32
    )
    return tile_masked(observed.astype(jnp.float32) - predicted, tile_flags).astype(jnp.bfloat16)


def transposed_product(first_operand, second_operand):
    return lax.dot_general(
        first_operand, second_operand, (((0,), (0,)), ((), ())), preferred_element_type=jnp.float32
    )


def advance(factors, gradient, rate):
    return (factors.astype(jnp.float32) + rate * gradient).astype(jnp.bfloat16)


def xor_pairs(count, bit):
    return [(i, i ^ (1 << bit)) for i in range(count)]


def halving_scatter(parts, axis, count, position, bits=None):
    steps = count.bit_length() - 1
    offsets = [0 for _ in parts]
    for bit in range(steps) if bits is None else bits:
        side = (position >> bit) & 1
        halves = [p.shape[0] // 2 for p in parts]
        kept = [lax.dynamic_slice_in_dim(p, side * h, h, 0) for p, h in zip(parts, halves)]
        sent = [lax.dynamic_slice_in_dim(p, (1 - side) * h, h, 0) for p, h in zip(parts, halves)]
        got = lax.ppermute(tuple(sent), axis, xor_pairs(count, bit))
        parts = [k + g for k, g in zip(kept, got)]
        offsets = [o + side * h for o, h in zip(offsets, halves)]
    return parts, offsets


def doubling_gather(parts, axis, count, position, bits=None):
    steps = count.bit_length() - 1
    for bit in reversed(range(steps)) if bits is None else bits:
        side = (position >> bit) & 1
        got = lax.ppermute(tuple(parts), axis, xor_pairs(count, bit))
        parts = [
            jnp.where(side == 0, jnp.concatenate([m, g], 0), jnp.concatenate([g, m], 0))
            for m, g in zip(parts, got)
        ]
    return parts


def shards(user_factors, item_factors, tag_factors, ratings, rating_tiles, tag_links, link_tiles):
    group_count = lax.axis_size("group")
    loop_count = lax.axis_size("loop")
    group_position = lax.axis_index("group")
    loop_position = lax.axis_index("loop")

    link_errors = residual_of(tag_links, item_factors, tag_factors, link_tiles)
    rating_errors = residual_of(ratings, user_factors, item_factors, rating_tiles)
    user_part = jnp.dot(rating_errors, item_factors, preferred_element_type=jnp.float32)
    tag_part = transposed_product(link_errors, item_factors)
    joint_part = jnp.concatenate([user_part, tag_part], 0)

    item_part = transposed_product(rating_errors, user_factors) + jnp.dot(
        link_errors, tag_factors, preferred_element_type=jnp.float32
    )
    joint_part, item_part = lax.optimization_barrier((joint_part, item_part))
    (joint_share,), (joint_offset,) = halving_scatter(
        [joint_part], "loop", loop_count, loop_position
    )
    group_steps = group_count.bit_length() - 1
    group_bits = [bit for bit in range(group_steps) if bit != 1] + [1][: group_steps > 1]
    first_bits = group_bits[:2]
    first_rows = item_part.shape[0] >> len(first_bits)

    def group_first(item_part):
        (share,), (offset,) = halving_scatter(
            [item_part], "group", group_count, group_position, first_bits
        )
        return share, offset

    first_share, first_offset = lax.cond(
        group_position >= 0,
        group_first,
        lambda p: (jnp.zeros((first_rows, p.shape[1]), p.dtype), jnp.int32(0)),
        item_part,
    )
    (item_share,), (item_offset,) = halving_scatter(
        [first_share], "group", group_count, group_position, group_bits[2:]
    )
    item_offset = first_offset + item_offset
    fresh_items = advance(
        lax.dynamic_slice_in_dim(item_factors, item_offset, item_share.shape[0], 0),
        item_share,
        step_items,
    )
    gather_bits = list(reversed(group_bits))
    (partly,) = doubling_gather(
        [fresh_items], "group", group_count, group_position, gather_bits[:1]
    )
    partly, joint_share = lax.optimization_barrier((partly, joint_share))
    joint_factors = jnp.concatenate([user_factors, tag_factors], 0)
    fresh_joint = advance(
        lax.dynamic_slice_in_dim(joint_factors, joint_offset, joint_share.shape[0], 0),
        joint_share,
        jnp.where(
            joint_offset + jnp.arange(joint_share.shape[0])[:, None] < user_factors.shape[0],
            step_users,
            step_tags,
        ),
    )
    (new_joint,) = doubling_gather([fresh_joint], "loop", loop_count, loop_position)
    new_users = new_joint[: user_factors.shape[0]]
    new_tags = new_joint[user_factors.shape[0] :]

    (partly,) = doubling_gather(
        [partly], "group", group_count, group_position, gather_bits[1:2]
    )
    partly, new_joint = lax.optimization_barrier((partly, new_joint))
    new_users = new_joint[: user_factors.shape[0]]
    new_tags = new_joint[user_factors.shape[0] :]
    (new_items,) = doubling_gather(
        [partly], "group", group_count, group_position, gather_bits[2:]
    )
    return (new_users, new_items, new_tags)


def solution(mesh):
    in_specs = (
        P("group", None),
        P("loop", None),
        P("group", None),
        P("group", "loop"),
        P("group", "loop"),
        P("loop", "group"),
        P("loop", "group"),
    )
    out_specs = (P("group", None), P("loop", None), P("group", None))
    return jax.shard_map(shards, mesh=mesh, in_specs=in_specs, out_specs=out_specs, check_vma=False)
```

```python
import jax
import jax.numpy as jnp
from jax import lax
from jax.sharding import PartitionSpec as P

step_users = 0.015
step_items = 0.004
step_tags = 0.015


def tile_masked(values, tile_flags):
    height, breadth = values.shape
    blocks = values.reshape(height // 128, 128, breadth // 128, 128)
    masked = blocks * tile_flags.astype(jnp.float32)[:, None, :, None]
    return masked.reshape(height, breadth)


def residual_of(observed, row_factors, column_factors, tile_flags):
    predicted = lax.dot_general(
        row_factors, column_factors, (((1,), (1,)), ((), ())), preferred_element_type=jnp.float32
    )
    return tile_masked(observed.astype(jnp.float32) - predicted, tile_flags).astype(jnp.bfloat16)


def transposed_product(first_operand, second_operand):
    return lax.dot_general(
        first_operand, second_operand, (((0,), (0,)), ((), ())), preferred_element_type=jnp.float32
    )


def advance(factors, gradient, rate):
    return (factors.astype(jnp.float32) + rate * gradient).astype(jnp.bfloat16)


def xor_pairs(count, bit):
    return [(i, i ^ (1 << bit)) for i in range(count)]


def halving_scatter(parts, axis, count, position, bits=None):
    steps = count.bit_length() - 1
    offsets = [0 for _ in parts]
    for bit in range(steps) if bits is None else bits:
        side = (position >> bit) & 1
        halves = [p.shape[0] // 2 for p in parts]
        kept = [lax.dynamic_slice_in_dim(p, side * h, h, 0) for p, h in zip(parts, halves)]
        sent = [lax.dynamic_slice_in_dim(p, (1 - side) * h, h, 0) for p, h in zip(parts, halves)]
        got = lax.ppermute(tuple(sent), axis, xor_pairs(count, bit))
        parts = [k + g for k, g in zip(kept, got)]
        offsets = [o + side * h for o, h in zip(offsets, halves)]
    return parts, offsets


def doubling_gather(parts, axis, count, position, bits=None):
    steps = count.bit_length() - 1
    for bit in reversed(range(steps)) if bits is None else bits:
        side = (position >> bit) & 1
        got = lax.ppermute(tuple(parts), axis, xor_pairs(count, bit))
        parts = [
            jnp.where(side == 0, jnp.concatenate([m, g], 0), jnp.concatenate([g, m], 0))
            for m, g in zip(parts, got)
        ]
    return parts


def shards(user_factors, item_factors, tag_factors, ratings, rating_tiles, tag_links, link_tiles):
    group_count = lax.axis_size("group")
    loop_count = lax.axis_size("loop")
    group_position = lax.axis_index("group")
    loop_position = lax.axis_index("loop")

    link_errors = residual_of(tag_links, item_factors, tag_factors, link_tiles)
    rating_errors = residual_of(ratings, user_factors, item_factors, rating_tiles)
    user_part = jnp.dot(rating_errors, item_factors, preferred_element_type=jnp.float32)
    tag_part = transposed_product(link_errors, item_factors)
    joint_part = jnp.concatenate([user_part, tag_part], 0)

    item_part = transposed_product(rating_errors, user_factors) + jnp.dot(
        link_errors, tag_factors, preferred_element_type=jnp.float32
    )
    joint_part, item_part = lax.optimization_barrier((joint_part, item_part))
    (joint_share,), (joint_offset,) = halving_scatter(
        [joint_part], "loop", loop_count, loop_position
    )
    group_steps = group_count.bit_length() - 1
    first_bits = list(range(min(2, group_steps)))
    first_rows = item_part.shape[0] >> len(first_bits)

    def group_first(item_part):
        (share,), (offset,) = halving_scatter(
            [item_part], "group", group_count, group_position, first_bits
        )
        return share, offset

    first_share, first_offset = lax.cond(
        group_position >= 0,
        group_first,
        lambda p: (jnp.zeros((first_rows, p.shape[1]), p.dtype), jnp.int32(0)),
        item_part,
    )
    (item_share,), (item_offset,) = halving_scatter(
        [first_share], "group", group_count, group_position, range(len(first_bits), group_steps)
    )
    item_offset = first_offset + item_offset
    fresh_items = advance(
        lax.dynamic_slice_in_dim(item_factors, item_offset, item_share.shape[0], 0),
        item_share,
        step_items,
    )
    gather_bits = list(reversed(range(group_steps)))
    (partly,) = doubling_gather(
        [fresh_items], "group", group_count, group_position, gather_bits[:1]
    )
    partly, joint_share = lax.optimization_barrier((partly, joint_share))
    joint_factors = jnp.concatenate([user_factors, tag_factors], 0)
    fresh_joint = advance(
        lax.dynamic_slice_in_dim(joint_factors, joint_offset, joint_share.shape[0], 0),
        joint_share,
        jnp.where(
            joint_offset + jnp.arange(joint_share.shape[0])[:, None] < user_factors.shape[0],
            step_users,
            step_tags,
        ),
    )
    (new_joint,) = doubling_gather([fresh_joint], "loop", loop_count, loop_position)
    new_users = new_joint[: user_factors.shape[0]]
    new_tags = new_joint[user_factors.shape[0] :]

    partly, _ = lax.optimization_barrier((partly, fresh_joint))
    (partly,) = doubling_gather(
        [partly], "group", group_count, group_position, gather_bits[1:-1]
    )
    partly, new_joint = lax.optimization_barrier((partly, new_joint))
    new_users = new_joint[: user_factors.shape[0]]
    new_tags = new_joint[user_factors.shape[0] :]
    (new_items,) = doubling_gather(
        [partly], "group", group_count, group_position, gather_bits[-1:]
    )
    return (new_users, new_items, new_tags)


def solution(mesh):
    in_specs = (
        P("group", None),
        P("loop", None),
        P("group", None),
        P("group", "loop"),
        P("group", "loop"),
        P("loop", "group"),
        P("loop", "group"),
    )
    out_specs = (P("group", None), P("loop", None), P("group", None))
    return jax.shard_map(shards, mesh=mesh, in_specs=in_specs, out_specs=out_specs, check_vma=False)
```

```python
import jax
import jax.numpy as jnp
from jax import lax
from jax.sharding import PartitionSpec as P

step_users = 0.015
step_items = 0.004
step_tags = 0.015


def tile_masked(values, tile_flags):
    height, breadth = values.shape
    blocks = values.reshape(height // 128, 128, breadth // 128, 128)
    masked = blocks * tile_flags.astype(jnp.float32)[:, None, :, None]
    return masked.reshape(height, breadth)


def residual_of(observed, row_factors, column_factors, tile_flags):
    predicted = lax.dot_general(
        row_factors, column_factors, (((1,), (1,)), ((), ())), preferred_element_type=jnp.float32
    )
    return tile_masked(observed.astype(jnp.float32) - predicted, tile_flags).astype(jnp.bfloat16)


def transposed_product(first_operand, second_operand):
    return lax.dot_general(
        first_operand, second_operand, (((0,), (0,)), ((), ())), preferred_element_type=jnp.float32
    )


def advance(factors, gradient, rate):
    return (factors.astype(jnp.float32) + rate * gradient).astype(jnp.bfloat16)


def xor_pairs(count, bit):
    return [(i, i ^ (1 << bit)) for i in range(count)]


def halving_scatter(parts, axis, count, position, bits=None):
    steps = count.bit_length() - 1
    offsets = [0 for _ in parts]
    for bit in range(steps) if bits is None else bits:
        side = (position >> bit) & 1
        halves = [p.shape[0] // 2 for p in parts]
        kept = [lax.dynamic_slice_in_dim(p, side * h, h, 0) for p, h in zip(parts, halves)]
        sent = [lax.dynamic_slice_in_dim(p, (1 - side) * h, h, 0) for p, h in zip(parts, halves)]
        got = lax.ppermute(tuple(sent), axis, xor_pairs(count, bit))
        parts = [k + g for k, g in zip(kept, got)]
        offsets = [o + side * h for o, h in zip(offsets, halves)]
    return parts, offsets


def doubling_gather(parts, axis, count, position, bits=None):
    steps = count.bit_length() - 1
    for bit in reversed(range(steps)) if bits is None else bits:
        side = (position >> bit) & 1
        got = lax.ppermute(tuple(parts), axis, xor_pairs(count, bit))
        parts = [
            jnp.concatenate([jnp.where(side == 0, m, g), jnp.where(side == 0, g, m)], 0)
            for m, g in zip(parts, got)
        ]
    return parts


def shards(user_factors, item_factors, tag_factors, ratings, rating_tiles, tag_links, link_tiles):
    group_count = lax.axis_size("group")
    loop_count = lax.axis_size("loop")
    group_position = lax.axis_index("group")
    loop_position = lax.axis_index("loop")

    link_errors = residual_of(tag_links, item_factors, tag_factors, link_tiles)
    rating_errors = residual_of(ratings, user_factors, item_factors, rating_tiles)
    user_part = jnp.dot(rating_errors, item_factors, preferred_element_type=jnp.float32)
    tag_part = transposed_product(link_errors, item_factors)
    joint_part = jnp.concatenate([user_part, tag_part], 0)

    item_part = transposed_product(rating_errors, user_factors) + jnp.dot(
        link_errors, tag_factors, preferred_element_type=jnp.float32
    )
    joint_part, item_part = lax.optimization_barrier((joint_part, item_part))
    (joint_share,), (joint_offset,) = halving_scatter(
        [joint_part], "loop", loop_count, loop_position
    )
    group_steps = group_count.bit_length() - 1
    first_bits = list(range(min(2, group_steps)))
    first_rows = item_part.shape[0] >> len(first_bits)

    def group_first(item_part):
        (share,), (offset,) = halving_scatter(
            [item_part], "group", group_count, group_position, first_bits
        )
        return share, offset

    first_share, first_offset = lax.cond(
        group_position >= 0,
        group_first,
        lambda p: (jnp.zeros((first_rows, p.shape[1]), p.dtype), jnp.int32(0)),
        item_part,
    )
    (item_share,), (item_offset,) = halving_scatter(
        [first_share], "group", group_count, group_position, range(len(first_bits), group_steps)
    )
    item_offset = first_offset + item_offset
    fresh_items = advance(
        lax.dynamic_slice_in_dim(item_factors, item_offset, item_share.shape[0], 0),
        item_share,
        step_items,
    )
    gather_bits = list(reversed(range(group_steps)))
    (partly,) = doubling_gather(
        [fresh_items], "group", group_count, group_position, gather_bits[:1]
    )
    partly, joint_share = lax.optimization_barrier((partly, joint_share))
    joint_factors = jnp.concatenate([user_factors, tag_factors], 0)
    fresh_joint = advance(
        lax.dynamic_slice_in_dim(joint_factors, joint_offset, joint_share.shape[0], 0),
        joint_share,
        jnp.where(
            joint_offset + jnp.arange(joint_share.shape[0])[:, None] < user_factors.shape[0],
            step_users,
            step_tags,
        ),
    )
    if loop_count == 2:
        other = lax.ppermute(fresh_joint, "loop", [(0, 1), (1, 0)])
        low = jnp.where(loop_position == 0, fresh_joint, other)
        high = jnp.where(loop_position == 0, other, fresh_joint)
        spill = user_factors.shape[0] - low.shape[0]
        new_joint = (jnp.concatenate([low, high[:spill]], 0), high[spill:])
    else:
        (new_joint,) = doubling_gather([fresh_joint], "loop", loop_count, loop_position)
        new_joint = (new_joint[: user_factors.shape[0]], new_joint[user_factors.shape[0] :])

    partly, _ = lax.optimization_barrier((partly, fresh_joint))
    (partly,) = doubling_gather(
        [partly], "group", group_count, group_position, gather_bits[1:-1]
    )
    partly, (new_users, new_tags) = lax.optimization_barrier((partly, new_joint))
    (new_items,) = doubling_gather(
        [partly], "group", group_count, group_position, gather_bits[-1:]
    )
    return (new_users, new_items, new_tags)


def solution(mesh):
    in_specs = (
        P("group", None),
        P("loop", None),
        P("group", None),
        P("group", "loop"),
        P("group", "loop"),
        P("loop", "group"),
        P("loop", "group"),
    )
    out_specs = (P("group", None), P("loop", None), P("group", None))
    return jax.shard_map(shards, mesh=mesh, in_specs=in_specs, out_specs=out_specs, check_vma=False)
```

```python
import jax
import jax.numpy as jnp
from jax import lax
from jax.sharding import PartitionSpec as P

step_users = 0.015
step_items = 0.004
step_tags = 0.015


def tile_masked(values, tile_flags):
    height, breadth = values.shape
    blocks = values.reshape(height // 128, 128, breadth // 128, 128)
    masked = blocks * tile_flags.astype(jnp.float32)[:, None, :, None]
    return masked.reshape(height, breadth)


def residual_of(observed, row_factors, column_factors, tile_flags):
    predicted = lax.dot_general(
        row_factors, column_factors, (((1,), (1,)), ((), ())), preferred_element_type=jnp.float32
    )
    return tile_masked(observed.astype(jnp.float32) - predicted, tile_flags).astype(jnp.bfloat16)


def transposed_product(first_operand, second_operand):
    return lax.dot_general(
        first_operand, second_operand, (((0,), (0,)), ((), ())), preferred_element_type=jnp.float32
    )


def advance(factors, gradient, rate):
    return (factors.astype(jnp.float32) + rate * gradient).astype(jnp.bfloat16)


def xor_pairs(count, bit):
    return [(i, i ^ (1 << bit)) for i in range(count)]


def halving_scatter(parts, axis, count, position, bits=None):
    steps = count.bit_length() - 1
    offsets = [0 for _ in parts]
    for bit in range(steps) if bits is None else bits:
        side = (position >> bit) & 1
        halves = [p.shape[0] // 2 for p in parts]
        kept = [lax.dynamic_slice_in_dim(p, side * h, h, 0) for p, h in zip(parts, halves)]
        sent = [lax.dynamic_slice_in_dim(p, (1 - side) * h, h, 0) for p, h in zip(parts, halves)]
        got = lax.ppermute(tuple(sent), axis, xor_pairs(count, bit))
        parts = [k + g for k, g in zip(kept, got)]
        offsets = [o + side * h for o, h in zip(offsets, halves)]
    return parts, offsets


def doubling_gather(parts, axis, count, position, bits=None):
    steps = count.bit_length() - 1
    for bit in reversed(range(steps)) if bits is None else bits:
        side = (position >> bit) & 1
        got = lax.ppermute(tuple(parts), axis, xor_pairs(count, bit))
        parts = [
            jnp.where(side == 0, jnp.concatenate([m, g], 0), jnp.concatenate([g, m], 0))
            for m, g in zip(parts, got)
        ]
    return parts


def shards(user_factors, item_factors, tag_factors, ratings, rating_tiles, tag_links, link_tiles):
    group_count = lax.axis_size("group")
    loop_count = lax.axis_size("loop")
    group_position = lax.axis_index("group")
    loop_position = lax.axis_index("loop")

    link_errors = residual_of(tag_links, item_factors, tag_factors, link_tiles)
    rating_errors = residual_of(ratings, user_factors, item_factors, rating_tiles)
    user_part = jnp.dot(rating_errors, item_factors, preferred_element_type=jnp.float32)
    tag_part = transposed_product(link_errors, item_factors)
    joint_part = jnp.concatenate([user_part, tag_part], 0)

    item_part = transposed_product(rating_errors, user_factors) + jnp.dot(
        link_errors, tag_factors, preferred_element_type=jnp.float32
    )
    joint_part, item_part = lax.optimization_barrier((joint_part, item_part))
    (joint_share,), (joint_offset,) = halving_scatter(
        [joint_part], "loop", loop_count, loop_position
    )
    group_steps = group_count.bit_length() - 1
    first_bits = list(range(min(2, group_steps)))
    first_rows = item_part.shape[0] >> len(first_bits)

    def group_first(item_part):
        (share,), (offset,) = halving_scatter(
            [item_part], "group", group_count, group_position, first_bits
        )
        return share, offset

    first_share, first_offset = lax.cond(
        group_position >= 0,
        group_first,
        lambda p: (jnp.zeros((first_rows, p.shape[1]), p.dtype), jnp.int32(0)),
        item_part,
    )
    (item_share,), (item_offset,) = halving_scatter(
        [first_share], "group", group_count, group_position, range(len(first_bits), group_steps)
    )
    item_offset = first_offset + item_offset
    fresh_items = advance(
        lax.dynamic_slice_in_dim(item_factors, item_offset, item_share.shape[0], 0),
        item_share,
        step_items,
    )
    gather_bits = list(reversed(range(group_steps)))
    (partly,) = doubling_gather(
        [fresh_items], "group", group_count, group_position, gather_bits[:1]
    )
    partly, joint_share = lax.optimization_barrier((partly, joint_share))
    joint_factors = jnp.concatenate([user_factors, tag_factors], 0)
    fresh_joint = advance(
        lax.dynamic_slice_in_dim(joint_factors, joint_offset, joint_share.shape[0], 0),
        joint_share,
        jnp.where(
            joint_offset + jnp.arange(joint_share.shape[0])[:, None] < user_factors.shape[0],
            step_users,
            step_tags,
        ),
    )
    if loop_count == 2:
        other = lax.ppermute(fresh_joint, "loop", [(0, 1), (1, 0)])
        low = jnp.where(loop_position == 0, fresh_joint, other)
        high = jnp.where(loop_position == 0, other, fresh_joint)
        spill = user_factors.shape[0] - low.shape[0]
        new_joint = (jnp.concatenate([low, high[:spill]], 0), high[spill:])
    else:
        (new_joint,) = doubling_gather([fresh_joint], "loop", loop_count, loop_position)
        new_joint = (new_joint[: user_factors.shape[0]], new_joint[user_factors.shape[0] :])

    partly, _ = lax.optimization_barrier((partly, fresh_joint))
    (partly,) = doubling_gather(
        [partly], "group", group_count, group_position, gather_bits[1:-1]
    )
    partly, (new_users, new_tags) = lax.optimization_barrier((partly, new_joint))
    (new_items,) = doubling_gather(
        [partly], "group", group_count, group_position, gather_bits[-1:]
    )
    return (new_users, new_items, new_tags)


def solution(mesh):
    in_specs = (
        P("group", None),
        P("loop", None),
        P("group", None),
        P("group", "loop"),
        P("group", "loop"),
        P("loop", "group"),
        P("loop", "group"),
    )
    out_specs = (P("group", None), P("loop", None), P("group", None))
    return jax.shard_map(shards, mesh=mesh, in_specs=in_specs, out_specs=out_specs, check_vma=False)
```

```python
import jax
import jax.numpy as jnp
from jax import lax
from jax.sharding import PartitionSpec as P

step_users = 0.015
step_items = 0.004
step_tags = 0.015


def tile_masked(values, tile_flags):
    height, breadth = values.shape
    blocks = values.reshape(height // 128, 128, breadth // 128, 128)
    masked = blocks * tile_flags.astype(jnp.float32)[:, None, :, None]
    return masked.reshape(height, breadth)


def residual_of(observed, row_factors, column_factors, tile_flags):
    predicted = lax.dot_general(
        row_factors, column_factors, (((1,), (1,)), ((), ())), preferred_element_type=jnp.float32
    )
    return tile_masked(observed.astype(jnp.float32) - predicted, tile_flags).astype(jnp.bfloat16)


def transposed_product(first_operand, second_operand):
    return lax.dot_general(
        first_operand, second_operand, (((0,), (0,)), ((), ())), preferred_element_type=jnp.float32
    )


def advance(factors, gradient, rate):
    return (factors.astype(jnp.float32) + rate * gradient).astype(jnp.bfloat16)


def xor_pairs(count, bit):
    return [(i, i ^ (1 << bit)) for i in range(count)]


def halving_scatter(parts, axis, count, position, bits=None):
    steps = count.bit_length() - 1
    offsets = [0 for _ in parts]
    for bit in range(steps) if bits is None else bits:
        side = (position >> bit) & 1
        halves = [p.shape[0] // 2 for p in parts]
        kept = [lax.dynamic_slice_in_dim(p, side * h, h, 0) for p, h in zip(parts, halves)]
        sent = [lax.dynamic_slice_in_dim(p, (1 - side) * h, h, 0) for p, h in zip(parts, halves)]
        got = lax.ppermute(tuple(sent), axis, xor_pairs(count, bit))
        parts = [k + g for k, g in zip(kept, got)]
        offsets = [o + side * h for o, h in zip(offsets, halves)]
    return parts, offsets


def doubling_gather(parts, axis, count, position, bits=None):
    steps = count.bit_length() - 1
    for bit in reversed(range(steps)) if bits is None else bits:
        side = (position >> bit) & 1
        got = lax.ppermute(tuple(parts), axis, xor_pairs(count, bit))
        parts = [
            jnp.where(side == 0, jnp.concatenate([m, g], 0), jnp.concatenate([g, m], 0))
            for m, g in zip(parts, got)
        ]
    return parts


def shards(user_factors, item_factors, tag_factors, ratings, rating_tiles, tag_links, link_tiles):
    group_count = lax.axis_size("group")
    loop_count = lax.axis_size("loop")
    group_position = lax.axis_index("group")
    loop_position = lax.axis_index("loop")

    link_errors = residual_of(tag_links, item_factors, tag_factors, link_tiles)
    rating_errors = residual_of(ratings, user_factors, item_factors, rating_tiles)
    user_part = jnp.dot(rating_errors, item_factors, preferred_element_type=jnp.float32)
    tag_part = transposed_product(link_errors, item_factors)
    joint_part = jnp.concatenate([user_part, tag_part], 0)

    item_part = transposed_product(rating_errors, user_factors) + jnp.dot(
        link_errors, tag_factors, preferred_element_type=jnp.float32
    )
    joint_part, item_part = lax.optimization_barrier((joint_part, item_part))
    (joint_share,), (joint_offset,) = halving_scatter(
        [joint_part], "loop", loop_count, loop_position
    )
    group_steps = group_count.bit_length() - 1
    first_bits = list(range(min(2, group_steps)))
    first_rows = item_part.shape[0] >> len(first_bits)

    def group_first(item_part):
        (share,), (offset,) = halving_scatter(
            [item_part], "group", group_count, group_position, first_bits
        )
        return share, offset

    first_share, first_offset = lax.cond(
        group_position >= 0,
        group_first,
        lambda p: (jnp.zeros((first_rows, p.shape[1]), p.dtype), jnp.int32(0)),
        item_part,
    )
    (item_share,), (item_offset,) = halving_scatter(
        [first_share], "group", group_count, group_position, range(len(first_bits), group_steps)
    )
    item_offset = first_offset + item_offset
    fresh_items = advance(
        lax.dynamic_slice_in_dim(item_factors, item_offset, item_share.shape[0], 0),
        item_share,
        step_items,
    )
    gather_bits = list(reversed(range(group_steps)))
    fresh_items, joint_share = lax.optimization_barrier((fresh_items, joint_share))
    joint_factors = jnp.concatenate([user_factors, tag_factors], 0)
    fresh_joint = advance(
        lax.dynamic_slice_in_dim(joint_factors, joint_offset, joint_share.shape[0], 0),
        joint_share,
        jnp.where(
            joint_offset + jnp.arange(joint_share.shape[0])[:, None] < user_factors.shape[0],
            step_users,
            step_tags,
        ),
    )
    (new_joint,) = doubling_gather([fresh_joint], "loop", loop_count, loop_position)
    partly, _ = lax.optimization_barrier((fresh_items, fresh_joint))
    (partly,) = doubling_gather(
        [partly], "group", group_count, group_position, gather_bits[:-1]
    )
    partly, new_joint = lax.optimization_barrier((partly, new_joint))
    new_users = new_joint[: user_factors.shape[0]]
    new_tags = new_joint[user_factors.shape[0] :]
    (new_items,) = doubling_gather(
        [partly], "group", group_count, group_position, gather_bits[-1:]
    )
    return (new_users, new_items, new_tags)


def solution(mesh):
    in_specs = (
        P("group", None),
        P("loop", None),
        P("group", None),
        P("group", "loop"),
        P("group", "loop"),
        P("loop", "group"),
        P("loop", "group"),
    )
    out_specs = (P("group", None), P("loop", None), P("group", None))
    return jax.shard_map(shards, mesh=mesh, in_specs=in_specs, out_specs=out_specs, check_vma=False)
```

```python
import jax
import jax.numpy as jnp
from jax import lax
from jax.sharding import PartitionSpec as P

step_users = 0.015
step_items = 0.004
step_tags = 0.015


def tile_masked(values, tile_flags):
    height, breadth = values.shape
    blocks = values.reshape(height // 128, 128, breadth // 128, 128)
    masked = blocks * tile_flags.astype(jnp.float32)[:, None, :, None]
    return masked.reshape(height, breadth)


def residual_of(observed, row_factors, column_factors, tile_flags):
    predicted = lax.dot_general(
        row_factors, column_factors, (((1,), (1,)), ((), ())), preferred_element_type=jnp.float32
    )
    return tile_masked(observed.astype(jnp.float32) - predicted, tile_flags).astype(jnp.bfloat16)


def transposed_product(first_operand, second_operand):
    return lax.dot_general(
        first_operand, second_operand, (((0,), (0,)), ((), ())), preferred_element_type=jnp.float32
    )


def advance(factors, gradient, rate):
    return (factors.astype(jnp.float32) + rate * gradient).astype(jnp.bfloat16)


def xor_pairs(count, bit):
    return [(i, i ^ (1 << bit)) for i in range(count)]


def halving_scatter(parts, axis, count, position, bits=None):
    steps = count.bit_length() - 1
    offsets = [0 for _ in parts]
    for bit in range(steps) if bits is None else bits:
        side = (position >> bit) & 1
        halves = [p.shape[0] // 2 for p in parts]
        kept = [lax.dynamic_slice_in_dim(p, side * h, h, 0) for p, h in zip(parts, halves)]
        sent = [lax.dynamic_slice_in_dim(p, (1 - side) * h, h, 0) for p, h in zip(parts, halves)]
        got = lax.ppermute(tuple(sent), axis, xor_pairs(count, bit))
        parts = [k + g for k, g in zip(kept, got)]
        offsets = [o + side * h for o, h in zip(offsets, halves)]
    return parts, offsets


def doubling_gather(parts, axis, count, position, bits=None, select_halves=False):
    steps = count.bit_length() - 1
    for bit in reversed(range(steps)) if bits is None else bits:
        side = (position >> bit) & 1
        got = lax.ppermute(tuple(parts), axis, xor_pairs(count, bit))
        if select_halves:
            parts = [
                jnp.concatenate([jnp.where(side == 0, m, g), jnp.where(side == 0, g, m)], 0)
                for m, g in zip(parts, got)
            ]
        else:
            parts = [
                jnp.where(side == 0, jnp.concatenate([m, g], 0), jnp.concatenate([g, m], 0))
                for m, g in zip(parts, got)
            ]
    return parts


def shards(user_factors, item_factors, tag_factors, ratings, rating_tiles, tag_links, link_tiles):
    group_count = lax.axis_size("group")
    loop_count = lax.axis_size("loop")
    group_position = lax.axis_index("group")
    loop_position = lax.axis_index("loop")

    link_errors = residual_of(tag_links, item_factors, tag_factors, link_tiles)
    rating_errors = residual_of(ratings, user_factors, item_factors, rating_tiles)
    user_part = jnp.dot(rating_errors, item_factors, preferred_element_type=jnp.float32)
    tag_part = transposed_product(link_errors, item_factors)
    joint_part = jnp.concatenate([user_part, tag_part], 0)

    item_part = transposed_product(rating_errors, user_factors) + jnp.dot(
        link_errors, tag_factors, preferred_element_type=jnp.float32
    )
    joint_part, item_part = lax.optimization_barrier((joint_part, item_part))
    (joint_share,), (joint_offset,) = halving_scatter(
        [joint_part], "loop", loop_count, loop_position
    )
    group_steps = group_count.bit_length() - 1
    first_bits = list(range(min(2, group_steps)))
    first_rows = item_part.shape[0] >> len(first_bits)

    def group_first(item_part):
        (share,), (offset,) = halving_scatter(
            [item_part], "group", group_count, group_position, first_bits
        )
        return share, offset

    first_share, first_offset = lax.cond(
        group_position >= 0,
        group_first,
        lambda p: (jnp.zeros((first_rows, p.shape[1]), p.dtype), jnp.int32(0)),
        item_part,
    )
    (item_share,), (item_offset,) = halving_scatter(
        [first_share], "group", group_count, group_position, range(len(first_bits), group_steps)
    )
    item_offset = first_offset + item_offset
    fresh_items = advance(
        lax.dynamic_slice_in_dim(item_factors, item_offset, item_share.shape[0], 0),
        item_share,
        step_items,
    )
    gather_bits = list(reversed(range(group_steps)))
    (partly,) = doubling_gather(
        [fresh_items], "group", group_count, group_position, gather_bits[:1]
    )
    partly, joint_share = lax.optimization_barrier((partly, joint_share))
    joint_factors = jnp.concatenate([user_factors, tag_factors], 0)
    fresh_joint = advance(
        lax.dynamic_slice_in_dim(joint_factors, joint_offset, joint_share.shape[0], 0),
        joint_share,
        jnp.where(
            joint_offset + jnp.arange(joint_share.shape[0])[:, None] < user_factors.shape[0],
            step_users,
            step_tags,
        ),
    )
    (new_joint,) = doubling_gather([fresh_joint], "loop", loop_count, loop_position)
    new_users = new_joint[: user_factors.shape[0]]
    new_tags = new_joint[user_factors.shape[0] :]

    partly, _ = lax.optimization_barrier((partly, fresh_joint))
    (partly,) = doubling_gather(
        [partly], "group", group_count, group_position, gather_bits[1:-1]
    )
    partly, new_joint = lax.optimization_barrier((partly, new_joint))
    new_users = new_joint[: user_factors.shape[0]]
    new_tags = new_joint[user_factors.shape[0] :]
    (new_items,) = doubling_gather(
        [partly], "group", group_count, group_position, gather_bits[-1:], True
    )
    return (new_users, new_items, new_tags)


def solution(mesh):
    in_specs = (
        P("group", None),
        P("loop", None),
        P("group", None),
        P("group", "loop"),
        P("group", "loop"),
        P("loop", "group"),
        P("loop", "group"),
    )
    out_specs = (P("group", None), P("loop", None), P("group", None))
    return jax.shard_map(shards, mesh=mesh, in_specs=in_specs, out_specs=out_specs, check_vma=False)
```

```python
import jax
import jax.numpy as jnp
from jax import lax
from jax.sharding import PartitionSpec as P

step_users = 0.015
step_items = 0.004
step_tags = 0.015


def tile_masked(values, tile_flags):
    height, breadth = values.shape
    blocks = values.reshape(height // 128, 128, breadth // 128, 128)
    masked = blocks * tile_flags.astype(jnp.float32)[:, None, :, None]
    return masked.reshape(height, breadth)


def residual_of(observed, row_factors, column_factors, tile_flags):
    predicted = lax.dot_general(
        row_factors, column_factors, (((1,), (1,)), ((), ())), preferred_element_type=jnp.float32
    )
    return tile_masked(observed.astype(jnp.float32) - predicted, tile_flags).astype(jnp.bfloat16)


def transposed_product(first_operand, second_operand):
    return lax.dot_general(
        first_operand, second_operand, (((0,), (0,)), ((), ())), preferred_element_type=jnp.float32
    )


def advance(factors, gradient, rate):
    return (factors.astype(jnp.float32) + rate * gradient).astype(jnp.bfloat16)


def xor_pairs(count, bit):
    return [(i, i ^ (1 << bit)) for i in range(count)]


def halving_scatter(parts, axis, count, position, bits=None):
    steps = count.bit_length() - 1
    offsets = [0 for _ in parts]
    for bit in range(steps) if bits is None else bits:
        side = (position >> bit) & 1
        halves = [p.shape[0] // 2 for p in parts]
        kept = [lax.dynamic_slice_in_dim(p, side * h, h, 0) for p, h in zip(parts, halves)]
        sent = [lax.dynamic_slice_in_dim(p, (1 - side) * h, h, 0) for p, h in zip(parts, halves)]
        got = lax.ppermute(tuple(sent), axis, xor_pairs(count, bit))
        parts = [k + g for k, g in zip(kept, got)]
        offsets = [o + side * h for o, h in zip(offsets, halves)]
    return parts, offsets


def doubling_gather(parts, axis, count, position, bits=None, select_halves=False):
    steps = count.bit_length() - 1
    for bit in reversed(range(steps)) if bits is None else bits:
        side = (position >> bit) & 1
        got = lax.ppermute(tuple(parts), axis, xor_pairs(count, bit))
        if select_halves:
            parts = [
                jnp.concatenate([jnp.where(side == 0, m, g), jnp.where(side == 0, g, m)], 0)
                for m, g in zip(parts, got)
            ]
        else:
            parts = [
                jnp.where(side == 0, jnp.concatenate([m, g], 0), jnp.concatenate([g, m], 0))
                for m, g in zip(parts, got)
            ]
    return parts


def shards(user_factors, item_factors, tag_factors, ratings, rating_tiles, tag_links, link_tiles):
    group_count = lax.axis_size("group")
    loop_count = lax.axis_size("loop")
    group_position = lax.axis_index("group")
    loop_position = lax.axis_index("loop")

    link_errors = residual_of(tag_links, item_factors, tag_factors, link_tiles)
    rating_errors = residual_of(ratings, user_factors, item_factors, rating_tiles)
    user_part = jnp.dot(rating_errors, item_factors, preferred_element_type=jnp.float32)
    tag_part = transposed_product(link_errors, item_factors)
    joint_part = jnp.concatenate([user_part, tag_part], 0)

    joint_part, rating_errors, link_errors = lax.optimization_barrier(
        (joint_part, rating_errors, link_errors)
    )
    (joint_share,), (joint_offset,) = halving_scatter(
        [joint_part], "loop", loop_count, loop_position
    )
    item_part = transposed_product(rating_errors, user_factors) + jnp.dot(
        link_errors, tag_factors, preferred_element_type=jnp.float32
    )
    item_part, _ = lax.optimization_barrier((item_part, rating_errors))
    group_steps = group_count.bit_length() - 1
    first_bits = list(range(min(2, group_steps)))
    first_rows = item_part.shape[0] >> len(first_bits)

    def group_first(item_part):
        (share,), (offset,) = halving_scatter(
            [item_part], "group", group_count, group_position, first_bits
        )
        return share, offset

    first_share, first_offset = lax.cond(
        group_position >= 0,
        group_first,
        lambda p: (jnp.zeros((first_rows, p.shape[1]), p.dtype), jnp.int32(0)),
        item_part,
    )
    (item_share,), (item_offset,) = halving_scatter(
        [first_share], "group", group_count, group_position, range(len(first_bits), group_steps)
    )
    item_offset = first_offset + item_offset
    fresh_items = advance(
        lax.dynamic_slice_in_dim(item_factors, item_offset, item_share.shape[0], 0),
        item_share,
        step_items,
    )
    gather_bits = list(reversed(range(group_steps)))
    (partly,) = doubling_gather(
        [fresh_items], "group", group_count, group_position, gather_bits[:1]
    )
    partly, joint_share = lax.optimization_barrier((partly, joint_share))
    joint_factors = jnp.concatenate([user_factors, tag_factors], 0)
    fresh_joint = advance(
        lax.dynamic_slice_in_dim(joint_factors, joint_offset, joint_share.shape[0], 0),
        joint_share,
        jnp.where(
            joint_offset + jnp.arange(joint_share.shape[0])[:, None] < user_factors.shape[0],
            step_users,
            step_tags,
        ),
    )
    (new_joint,) = doubling_gather([fresh_joint], "loop", loop_count, loop_position)
    new_users = new_joint[: user_factors.shape[0]]
    new_tags = new_joint[user_factors.shape[0] :]

    partly, _ = lax.optimization_barrier((partly, fresh_joint))
    (partly,) = doubling_gather(
        [partly], "group", group_count, group_position, gather_bits[1:-1]
    )
    partly, new_joint = lax.optimization_barrier((partly, new_joint))
    new_users = new_joint[: user_factors.shape[0]]
    new_tags = new_joint[user_factors.shape[0] :]
    (new_items,) = doubling_gather(
        [partly], "group", group_count, group_position, gather_bits[-1:], True
    )
    return (new_users, new_items, new_tags)


def solution(mesh):
    in_specs = (
        P("group", None),
        P("loop", None),
        P("group", None),
        P("group", "loop"),
        P("group", "loop"),
        P("loop", "group"),
        P("loop", "group"),
    )
    out_specs = (P("group", None), P("loop", None), P("group", None))
    return jax.shard_map(shards, mesh=mesh, in_specs=in_specs, out_specs=out_specs, check_vma=False)
```

```python
import jax
import jax.numpy as jnp
from jax import lax
from jax.sharding import PartitionSpec as P

step_users = 0.015
step_items = 0.004
step_tags = 0.015


def tile_masked(values, tile_flags):
    height, breadth = values.shape
    blocks = values.reshape(height // 128, 128, breadth // 128, 128)
    masked = blocks * tile_flags.astype(jnp.float32)[:, None, :, None]
    return masked.reshape(height, breadth)


def residual_of(observed, row_factors, column_factors, tile_flags):
    predicted = lax.dot_general(
        row_factors, column_factors, (((1,), (1,)), ((), ())), preferred_element_type=jnp.float32
    )
    return tile_masked(observed.astype(jnp.float32) - predicted, tile_flags).astype(jnp.bfloat16)


def transposed_product(first_operand, second_operand):
    return lax.dot_general(
        first_operand, second_operand, (((0,), (0,)), ((), ())), preferred_element_type=jnp.float32
    )


def advance(factors, gradient, rate):
    return (factors.astype(jnp.float32) + rate * gradient).astype(jnp.bfloat16)


def xor_pairs(count, bit):
    return [(i, i ^ (1 << bit)) for i in range(count)]


def halving_scatter(parts, axis, count, position, bits=None):
    steps = count.bit_length() - 1
    offsets = [0 for _ in parts]
    for bit in range(steps) if bits is None else bits:
        side = (position >> bit) & 1
        halves = [p.shape[0] // 2 for p in parts]
        kept = [lax.dynamic_slice_in_dim(p, side * h, h, 0) for p, h in zip(parts, halves)]
        sent = [lax.dynamic_slice_in_dim(p, (1 - side) * h, h, 0) for p, h in zip(parts, halves)]
        got = lax.ppermute(tuple(sent), axis, xor_pairs(count, bit))
        parts = [k + g for k, g in zip(kept, got)]
        offsets = [o + side * h for o, h in zip(offsets, halves)]
    return parts, offsets


def doubling_gather(parts, axis, count, position, bits=None, select_halves=False):
    steps = count.bit_length() - 1
    for bit in reversed(range(steps)) if bits is None else bits:
        side = (position >> bit) & 1
        got = lax.ppermute(tuple(parts), axis, xor_pairs(count, bit))
        if select_halves:
            parts = [
                jnp.concatenate([jnp.where(side == 0, m, g), jnp.where(side == 0, g, m)], 0)
                for m, g in zip(parts, got)
            ]
        else:
            parts = [
                jnp.where(side == 0, jnp.concatenate([m, g], 0), jnp.concatenate([g, m], 0))
                for m, g in zip(parts, got)
            ]
    return parts


def shards(user_factors, item_factors, tag_factors, ratings, rating_tiles, tag_links, link_tiles):
    group_count = lax.axis_size("group")
    loop_count = lax.axis_size("loop")
    group_position = lax.axis_index("group")
    loop_position = lax.axis_index("loop")

    link_errors = residual_of(tag_links, item_factors, tag_factors, link_tiles)
    rating_errors = residual_of(ratings, user_factors, item_factors, rating_tiles)
    user_part = jnp.dot(rating_errors, item_factors, preferred_element_type=jnp.float32)
    tag_part = transposed_product(link_errors, item_factors)
    joint_part = jnp.concatenate([user_part, tag_part], 0)

    item_part = transposed_product(rating_errors, user_factors) + jnp.dot(
        link_errors, tag_factors, preferred_element_type=jnp.float32
    )
    joint_part, item_part = lax.optimization_barrier((joint_part, item_part))
    (joint_share,), (joint_offset,) = halving_scatter(
        [joint_part], "loop", loop_count, loop_position
    )
    group_steps = group_count.bit_length() - 1
    first_bits = list(range(min(3, group_steps)))
    first_rows = item_part.shape[0] >> len(first_bits)

    def group_first(item_part):
        (share,), (offset,) = halving_scatter(
            [item_part], "group", group_count, group_position, first_bits
        )
        return share, offset

    first_share, first_offset = lax.cond(
        group_position >= 0,
        group_first,
        lambda p: (jnp.zeros((first_rows, p.shape[1]), p.dtype), jnp.int32(0)),
        item_part,
    )
    (item_share,), (item_offset,) = halving_scatter(
        [first_share], "group", group_count, group_position, range(len(first_bits), group_steps)
    )
    item_offset = first_offset + item_offset
    fresh_items = advance(
        lax.dynamic_slice_in_dim(item_factors, item_offset, item_share.shape[0], 0),
        item_share,
        step_items,
    )
    gather_bits = list(reversed(range(group_steps)))
    (partly,) = doubling_gather(
        [fresh_items], "group", group_count, group_position, gather_bits[:1]
    )
    partly, joint_share = lax.optimization_barrier((partly, joint_share))
    joint_factors = jnp.concatenate([user_factors, tag_factors], 0)
    fresh_joint = advance(
        lax.dynamic_slice_in_dim(joint_factors, joint_offset, joint_share.shape[0], 0),
        joint_share,
        jnp.where(
            joint_offset + jnp.arange(joint_share.shape[0])[:, None] < user_factors.shape[0],
            step_users,
            step_tags,
        ),
    )
    (new_joint,) = doubling_gather([fresh_joint], "loop", loop_count, loop_position)
    new_users = new_joint[: user_factors.shape[0]]
    new_tags = new_joint[user_factors.shape[0] :]

    partly, _ = lax.optimization_barrier((partly, fresh_joint))
    (partly,) = doubling_gather(
        [partly], "group", group_count, group_position, gather_bits[1:-1]
    )
    partly, new_joint = lax.optimization_barrier((partly, new_joint))
    new_users = new_joint[: user_factors.shape[0]]
    new_tags = new_joint[user_factors.shape[0] :]
    (new_items,) = doubling_gather(
        [partly], "group", group_count, group_position, gather_bits[-1:], True
    )
    return (new_users, new_items, new_tags)


def solution(mesh):
    in_specs = (
        P("group", None),
        P("loop", None),
        P("group", None),
        P("group", "loop"),
        P("group", "loop"),
        P("loop", "group"),
        P("loop", "group"),
    )
    out_specs = (P("group", None), P("loop", None), P("group", None))
    return jax.shard_map(shards, mesh=mesh, in_specs=in_specs, out_specs=out_specs, check_vma=False)
```
